128 devices in a mesh: ex: 8 (over z, core), sh: 16 (over y, x).
Axes of the slice: x: 4, y: 4, z: 4, core: 2. Of those that a mesh axis runs over, the one named last changes fastest.
Arguments:
- hidden_in: bfloat16 [12288, 2304], P(('ex', 'sh')), may hold values from -3 to 3
- queries: bfloat16 [12288, 2304], P(('ex', 'sh')), may hold values from -2.5 to 2.5
- new_keys: bfloat16 [12288, 2304], P(('ex', 'sh')), may hold values from -2.5 to 2.5
- new_values: bfloat16 [12288, 2304], P(('ex', 'sh')), may hold values from -6 to 6
- key_pool: bfloat16 [131072, 2304], P(('ex', 'sh')), may hold values from -2.5 to 2.5
- value_pool: bfloat16 [131072, 2304], P(('ex', 'sh')), may hold values from -6 to 6
- page_order: int32 [128, 64], P(('ex', 'sh')), may hold values from 0 to 63, each once within a row
- new_lengths: int32 [128, 4], P(('ex', 'sh')), may hold values from 1 to 48, 96 in all within a row
- context_lengths: int32 [128, 4], P(('ex', 'sh')), may hold values from 1 to 256, 512 in all within a row
- route_ids: int32 [12288, 2], P(('ex', 'sh')), may hold values from 0 to 7, all different within a row; in each aligned block of 96 rows (0 to 95, 96 to 191, ...) at most 32 rows name the same one
- norm_gain: bfloat16 [2304], replicated, may hold values from 0.25 to 1.75
- router_weight: bfloat16 [2304, 8], replicated, may hold values from -0.125 to 0.125
- gate_weight: bfloat16 [8, 2304, 5760], P('ex', None, 'sh'), may hold values from -0.125 to 0.125
- up_weight: bfloat16 [8, 2304, 5760], P('ex', None, 'sh'), may hold values from -0.125 to 0.125
- down_weight: bfloat16 [8, 5760, 2304], P('ex', 'sh'), may hold values from -0.078125 to 0.078125
- out_gain: bfloat16 [2304], replicated, may hold values from 0.25 to 1.75
Outputs:
- layer_out: bfloat16 [12288, 2304], P(('ex', 'sh'))
The draws below stay inside these ranges and needn't reach their ends.
Inputs may be any that keep to these rules, and one draw needn't show every extreme that they name: `page_order`: each row names the pages 0 to 63 of one device's pool once each; request r owns entries r * 16 to (r+1) * 16 - 1 of its row, in order. `new_lengths`: each row sums to 96; its largest entry is 48. `context_lengths`: each row sums to 512; its largest entry is 256. `route_ids`: A row names two different experts. Among the 96 rows of one device no expert is named by more than 32 rows, and in some devices' rows one expert is named by exactly 32.
All inputs are finite; a program needn't handle non-finite values.
Results may differ from the reference program's by a relative error of at most 0.015.
Values may be sent and summed in bfloat16 or wider, within the bound.
No kernel may reach another device: no remote copies, remote signals or barrier semaphores. Data moves between devices by JAX's collectives and lax.ppermute only.
A program may use at most 128 MiB of HBM per device.

```python
import math
import jax
import jax.numpy as jnp
import numpy as np
from jax import lax

D = 2304
HEADS = 36
HEAD_DIM = 64
FF = 5760
EXPERTS = 8
TOP = 2
TOK_DEV = 96
REQ_DEV = 4
PAGE = 16
PAGES_DEV = 64
BLOCKS = 128
TOKENS = 12288
POOL = 1024
CTX_MOST = 256
CTX_TOTAL = 512
NEW_MOST = 48
MOST = 32
FF_SLICE = 360
N_SH = 16


def steps_of(stream_key, shape, cuts, low, largest):
    factor_of, own = 1.0, jax.random.fold_in(stream_key, 6)
    for dim, parts in cuts:
        draws = jnp.exp(jax.random.uniform(jax.random.fold_in(own, dim), (parts,), jnp.float32, low / len(cuts), largest / len(cuts)))
        factor_of = factor_of * jnp.repeat(draws, shape[dim] // parts).reshape([-1 if axis == dim else 1 for axis in range(len(shape))])
    return factor_of


def split_up(amount, total, most, lean):
    weights = [(1 << 20) // math.isqrt(grade ** lean) + 1 for grade in range(2, amount + 1)]
    rest, counts = total - most - (amount - 1), [1] * (amount - 1)
    while rest > 0:
        movable = [i for i in range(amount - 1) if counts[i] < most]
        whole, budget = sum([weights[i] for i in movable]), rest
        for i in movable:
            more = min(most - counts[i], max(1, budget * weights[i] // whole), rest)
            counts[i] = counts[i] + more
            rest = rest - more
    return np.array([most] + counts)


def uneven_parts(key, amount, total, most, lean):
    if amount == 2:
        one = jax.random.randint(key, (), max(1, total - most), min(most, total - 1) + 1)
        return jnp.stack([one, total - one])
    sizes = jnp.asarray(split_up(amount, total, most, lean), jnp.int32)
    pairs = (amount - 1) // 2
    giver, sink = sizes[1:1 + 2 * pairs:2], sizes[2:2 + 2 * pairs:2]
    room = jnp.minimum(giver - 1, most - sink)
    moved = jax.random.randint(jax.random.fold_in(key, 1), (pairs,), 0, 1 << 20) % (room + 1)
    sizes = sizes.at[1:1 + 2 * pairs:2].set(giver - moved).at[2:2 + 2 * pairs:2].set(sink + moved)
    return sizes[jax.random.permutation(jax.random.fold_in(key, 2), amount)]


def shared_out(stream_key, own, number, rows, amount, top, limit, skew):
    sequence = jax.random.permutation(stream_key, amount)
    crowded, ordinary = load_shares(amount, rows * top, limit, skew, True), load_shares(amount, rows * top, limit, skew, False)
    places = jnp.arange(amount)

    def named(sizes, turn):
        used = int((sizes > 0).sum())
        fixed = max(1, used // 4)
        passed = fixed + (places - fixed + turn * (used - fixed)) % max(1, amount - fixed)
        return jnp.zeros((amount,), jnp.int32).at[sequence[jnp.where(places < fixed, places, passed)]].set(jnp.asarray(sizes, jnp.int32))

    sizes = jnp.where(number % 4 == 0, named(crowded, number // 4), named(ordinary, number - number // 4 - 1))
    mixed = jax.random.permutation(jax.random.fold_in(own, 3), amount)
    source_of, receiver = mixed[0:amount // 2 * 2:2], mixed[1:amount // 2 * 2:2]
    room = jnp.minimum(sizes[source_of] - 1, limit - sizes[receiver]) // 2
    room = jnp.where((source_of == sequence[0]) | (receiver == sequence[0]) | (sizes[receiver] == 0), 0, jnp.maximum(room, 0))
    passed = jax.random.randint(jax.random.fold_in(own, 4), (amount // 2,), 0, 1 << 20) % (room + 1)
    sizes = sizes.at[source_of].add(-passed).at[receiver].add(passed)
    members = jnp.searchsorted(jnp.cumsum(sizes), jnp.arange(rows * top), side="right").astype(jnp.int32)
    listing = members.reshape(top, rows).T
    listing = listing[jax.random.permutation(jax.random.fold_in(own, 1), rows)]
    turn = jax.random.randint(jax.random.fold_in(own, 2), (rows, 1), 0, top)
    return jnp.take_along_axis(listing, (jnp.arange(top)[None, :] + turn) % top, axis=1)


def load_shares(amount, total, reach, skew, full):
    portions = [(1 << 20) // math.isqrt(standing ** skew) + 1 for standing in range(1, amount + 1)]
    largest = reach if full else min(reach, max(-(-total // amount), total * portions[0] // sum(portions)))
    least = 1 if total - largest >= amount - 1 else 0
    given, spare = [largest] + [least] * (amount - 1), total - largest - least * (amount - 1)
    while spare > 0:
        free = [i for i in range(1, amount) if given[i] < largest] or [i for i in range(1, amount) if given[i] < reach]
        pool, left = sum([portions[i] for i in free]), spare
        for i in free:
            more = min(reach - given[i], max(1, left * portions[i] // pool), spare)
            given[i] = given[i] + more
            spare = spare - more
    return np.array(given)


def noise(own_key, shape, width, limit, cuts=(), kind=jnp.bfloat16):
    entries = width * jax.random.normal(own_key, shape, jnp.float32)
    if cuts:
        entries = entries * steps_of(own_key, shape, cuts, -0.22, 0.18)
    return jnp.clip(entries, -limit, limit).astype(kind)


def setup_inputs(seed: int = 0) -> dict:
    key_of = jax.random.split(jax.random.key(seed), 17)
    hidden_in = noise(key_of[0], (TOKENS, D), 0.5, 3.0, ((0, 128),))
    queries = noise(key_of[1], (TOKENS, D), 1.0, 2.5, ((0, 128),))
    new_keys = noise(key_of[2], (TOKENS, D), 1.0, 2.5, ((0, 128),))
    new_values = noise(key_of[3], (TOKENS, D), 1.5, 6.0, ((0, 128),))
    key_pool = noise(key_of[4], (BLOCKS * POOL, D), 1.0, 2.5, ((0, 128),))
    value_pool = noise(key_of[5], (BLOCKS * POOL, D), 1.5, 6.0, ((0, 128),))
    page_order = jax.vmap(lambda own: jax.random.permutation(own, PAGES_DEV))(jax.random.split(key_of[6], BLOCKS)).reshape((BLOCKS, PAGES_DEV)).astype(jnp.int32)
    new_lengths = jax.vmap(lambda own: uneven_parts(own, REQ_DEV, TOK_DEV, NEW_MOST, 1))(jax.random.split(key_of[7], BLOCKS)).reshape((BLOCKS, REQ_DEV)).astype(jnp.int32)
    context_lengths = jax.vmap(lambda own: uneven_parts(own, REQ_DEV, CTX_TOTAL, CTX_MOST, 2))(jax.random.split(key_of[8], BLOCKS)).reshape((BLOCKS, REQ_DEV)).astype(jnp.int32)
    route_ids_keys = jax.random.split(jax.random.fold_in(key_of[9], 1), TOKENS // TOK_DEV)
    route_ids_turns = jax.random.permutation(jax.random.fold_in(key_of[9], 3), TOKENS // TOK_DEV)
    route_ids = jax.vmap(lambda own, number: shared_out(jax.random.fold_in(key_of[9], 2), own, number, TOK_DEV, EXPERTS, TOP, MOST, 2))(route_ids_keys, route_ids_turns).reshape((TOKENS, TOP))
    norm_gain = jnp.clip(1.0 + 0.15 * jax.random.normal(key_of[10], (D,), jnp.float32), 0.25, 1.75).astype(jnp.bfloat16)
    router_weight = noise(key_of[11], (D, EXPERTS), D ** -0.5, 0.125)
    gate_weight = noise(key_of[12], (EXPERTS, D, FF), D ** -0.5, 0.125, ((0, 8), (2, 16)))
    up_weight = noise(key_of[13], (EXPERTS, D, FF), D ** -0.5, 0.125, ((0, 8), (2, 16)))
    down_weight = noise(key_of[14], (EXPERTS, FF, D), FF ** -0.5, 0.078125, ((0, 8), (1, 16)))
    out_gain = jnp.clip(1.0 + 0.15 * jax.random.normal(key_of[15], (D,), jnp.float32), 0.25, 1.75).astype(jnp.bfloat16)
    return {"hidden_in": hidden_in, "queries": queries, "new_keys": new_keys, "new_values": new_values, "key_pool": key_pool, "value_pool": value_pool, "page_order": page_order, "new_lengths": new_lengths, "context_lengths": context_lengths, "route_ids": route_ids, "norm_gain": norm_gain, "router_weight": router_weight, "gate_weight": gate_weight, "up_weight": up_weight, "down_weight": down_weight, "out_gain": out_gain}


def rms_scale(values, gain):
    mean_square = lax.optimization_barrier(jnp.mean(values * values, axis=-1, keepdims=True))
    return values * lax.rsqrt(mean_square + 1e-05) * gain.astype(jnp.float32)

def route_probs(normed, router_weight, route_ids):
    logits = jnp.dot(normed, router_weight, preferred_element_type=jnp.float32)
    expert_range = jnp.arange(router_weight.shape[1], dtype=jnp.int32)
    picked = lax.optimization_barrier(jnp.sum(jnp.where(route_ids[:, :, None] == expert_range[None, None, :], logits[:, None, :], 0.0), axis=2))
    raised = jnp.exp(picked)
    return raised / lax.optimization_barrier(jnp.sum(raised, axis=1, keepdims=True))

def attend(hidden_rows, query_rows, key_rows, value_rows, key_store, value_store, page_row, new_row_lengths, context_row_lengths):
    row_count = query_rows.shape[0]
    store_count = key_store.shape[0]
    requests = new_row_lengths.shape[0]
    table = page_row.reshape(requests, -1)
    per_request = table.shape[1]
    ends = jnp.cumsum(new_row_lengths).astype(jnp.int32)
    row_index = jnp.arange(row_count, dtype=jnp.int32)
    owner = lax.optimization_barrier(jnp.sum((row_index[:, None] >= ends[None, :]).astype(jnp.int32), axis=1)).astype(jnp.int32)
    request_index = jnp.arange(requests, dtype=jnp.int32)
    row_owner = owner[:, None] == request_index[None, :]
    token_index = jnp.arange(store_count, dtype=jnp.int32)
    token_page = token_index // PAGE
    token_offset = token_index % PAGE
    matched = table[:, :, None] == token_page[None, None, :]
    page_slot = jnp.arange(per_request, dtype=jnp.int32) * PAGE
    position = lax.optimization_barrier(jnp.sum(jnp.where(matched, page_slot[None, :, None], 0), axis=1)).astype(jnp.int32) + token_offset[None, :]
    visible = jnp.any(matched, axis=1) & (position < context_row_lengths[:, None])
    store_mask = jnp.any(row_owner[:, :, None] & visible[None, :, :], axis=1)
    fresh_mask = (owner[:, None] == owner[None, :]) & (row_index[None, :] <= row_index[:, None])
    allowed = jnp.concatenate([store_mask, fresh_mask], axis=1)
    keys = jnp.concatenate([key_store, key_rows], axis=0).reshape(-1, HEADS, HEAD_DIM).astype(jnp.float32)
    values = jnp.concatenate([value_store, value_rows], axis=0).reshape(-1, HEADS, HEAD_DIM).astype(jnp.float32)
    query_heads = query_rows.reshape(row_count, HEADS, HEAD_DIM).astype(jnp.float32)
    scores = jnp.einsum('rhd,khd->hrk', query_heads, keys) * HEAD_DIM ** (-0.5)
    raised = jnp.where(allowed[None, :, :], jnp.exp(scores), 0.0)
    weights = (raised / lax.optimization_barrier(jnp.sum(raised, axis=2, keepdims=True))).astype(jnp.bfloat16)
    attended = jnp.einsum('hrk,khd->rhd', weights.astype(jnp.float32), values).reshape(row_count, HEADS * HEAD_DIM)
    return hidden_rows.astype(jnp.float32) + attended

def reference(hidden_in, queries, new_keys, new_values, key_pool, value_pool, page_order, new_lengths, context_lengths, route_ids, norm_gain, router_weight, gate_weight, up_weight, down_weight, out_gain):

    def one_block(packed):
        return attend(*packed)
    blocked = (hidden_in.reshape(BLOCKS, TOK_DEV, D), queries.reshape(BLOCKS, TOK_DEV, D), new_keys.reshape(BLOCKS, TOK_DEV, D), new_values.reshape(BLOCKS, TOK_DEV, D), key_pool.reshape(BLOCKS, POOL, D), value_pool.reshape(BLOCKS, POOL, D), page_order, new_lengths, context_lengths)
    resid = lax.map(one_block, blocked).reshape(TOKENS, D)
    normed = rms_scale(resid, norm_gain).astype(jnp.bfloat16)
    route_weights = route_probs(normed, router_weight, route_ids)
    mixed = resid
    capacity = BLOCKS * MOST
    for expert in range(EXPERTS):
        chosen = route_ids == expert
        selected = jnp.any(chosen, axis=1)
        count = jnp.sum(selected.astype(jnp.int32)).astype(jnp.int32)
        index = jnp.nonzero(selected, size=capacity, fill_value=0)[0].astype(jnp.int32)
        valid = jnp.arange(capacity, dtype=jnp.int32) < count
        rows_in = normed[index]
        gate_value = jnp.dot(rows_in, gate_weight[expert], preferred_element_type=jnp.float32)
        up_value = jnp.dot(rows_in, up_weight[expert], preferred_element_type=jnp.float32)
        hidden = (jax.nn.silu(gate_value) * up_value).astype(jnp.bfloat16)
        down_expert = down_weight[expert]

        def add_part(part, total):
            start = (part * FF_SLICE).astype(jnp.int32)
            hidden_part = lax.dynamic_slice_in_dim(hidden, start, FF_SLICE, 1)
            down_part = lax.dynamic_slice_in_dim(down_expert, start, FF_SLICE, 0)
            term = jnp.dot(hidden_part, down_part, preferred_element_type=jnp.float32).astype(jnp.bfloat16)
            return total + term.astype(jnp.float32)
        summed = lax.fori_loop(0, N_SH, add_part, jnp.zeros((capacity, D), jnp.float32))
        expert_out = summed.astype(jnp.bfloat16)
        token_weight = lax.optimization_barrier(jnp.sum(jnp.where(chosen, route_weights, 0.0), axis=1))
        scale = jnp.where(valid, token_weight[index], 0.0)
        mixed = mixed.at[index].add(scale[:, None] * expert_out.astype(jnp.float32))
    return rms_scale(mixed, out_gain).astype(jnp.bfloat16)
```

```python
import jax
import jax.numpy as jnp
from jax import lax
from jax.sharding import PartitionSpec as P

HEADS = 36
HEAD_DIM = 64
EXPERTS = 8
PAGE = 16
MOST = 32


def rms_scale(values, gain):
    mean_square = jnp.mean(values * values, axis=-1, keepdims=True)
    return values * lax.rsqrt(mean_square + 1e-05) * gain.astype(jnp.float32)


def route_probs(normed, router_weight, route_ids):
    logits = jnp.dot(normed, router_weight, preferred_element_type=jnp.float32)
    expert_range = jnp.arange(router_weight.shape[1], dtype=jnp.int32)
    picked = jnp.sum(
        jnp.where(route_ids[:, :, None] == expert_range[None, None, :], logits[:, None, :], 0.0),
        axis=2,
    )
    raised = jnp.exp(picked)
    return raised / jnp.sum(raised, axis=1, keepdims=True)


def attend(
    hidden_rows,
    query_rows,
    key_rows,
    value_rows,
    key_store,
    value_store,
    page_row,
    new_row_lengths,
    context_row_lengths,
):
    row_count = query_rows.shape[0]
    store_count = key_store.shape[0]
    requests = new_row_lengths.shape[0]
    table = page_row.reshape(requests, -1)
    per_request = table.shape[1]
    ends = jnp.cumsum(new_row_lengths)
    row_index = jnp.arange(row_count, dtype=jnp.int32)
    owner = jnp.sum((row_index[:, None] >= ends[None, :]).astype(jnp.int32), axis=1)
    request_index = jnp.arange(requests, dtype=jnp.int32)
    row_owner = owner[:, None] == request_index[None, :]
    token_index = jnp.arange(store_count, dtype=jnp.int32)
    token_page = token_index // PAGE
    token_offset = token_index % PAGE
    matched = table[:, :, None] == token_page[None, None, :]
    page_slot = jnp.arange(per_request, dtype=jnp.int32) * PAGE
    position = (
        jnp.sum(jnp.where(matched, page_slot[None, :, None], 0), axis=1) + token_offset[None, :]
    )
    visible = jnp.any(matched, axis=1) & (position < context_row_lengths[:, None])
    store_mask = jnp.any(row_owner[:, :, None] & visible[None, :, :], axis=1)
    fresh_mask = (owner[:, None] == owner[None, :]) & (row_index[None, :] <= row_index[:, None])
    allowed = jnp.concatenate([store_mask, fresh_mask], axis=1)
    keys = jnp.concatenate([key_store, key_rows], axis=0).reshape(-1, HEADS, HEAD_DIM)
    values = jnp.concatenate([value_store, value_rows], axis=0).reshape(-1, HEADS, HEAD_DIM)
    query_heads = query_rows.reshape(row_count, HEADS, HEAD_DIM)
    scores = jnp.einsum(
        "rhd,khd->hrk", query_heads, keys, preferred_element_type=jnp.float32
    ) * HEAD_DIM ** (-0.5)
    raised = jnp.where(allowed[None, :, :], jnp.exp(scores), 0.0)
    weights = (raised / jnp.sum(raised, axis=2, keepdims=True)).astype(jnp.bfloat16)
    attended = jnp.einsum(
        "hrk,khd->rhd", weights, values, preferred_element_type=jnp.float32
    ).reshape(row_count, HEADS * HEAD_DIM)
    return hidden_rows.astype(jnp.float32) + attended


def per_device(
    hidden_in,
    queries,
    new_keys,
    new_values,
    key_pool,
    value_pool,
    page_order,
    new_lengths,
    context_lengths,
    route_ids,
    norm_gain,
    router_weight,
    gate_weight,
    up_weight,
    down_weight,
    out_gain,
):
    groups = lax.axis_size("ex")
    local_experts = gate_weight.shape[0]
    width = hidden_in.shape[1]
    row_count = hidden_in.shape[0]
    resid = attend(
        hidden_in,
        queries,
        new_keys,
        new_values,
        key_pool,
        value_pool,
        page_order[0],
        new_lengths[0],
        context_lengths[0],
    )
    normed = rms_scale(resid, norm_gain).astype(jnp.bfloat16)
    route_weights = route_probs(normed, router_weight, route_ids)
    top_count = route_ids.shape[1]
    entries = route_ids.reshape(-1)
    expert_range = jnp.arange(EXPERTS, dtype=jnp.int32)
    onehot = (entries[:, None] == expert_range[None, :]).astype(jnp.int32)
    before = jnp.cumsum(onehot, axis=0) - onehot
    slot_index = jnp.sum(before * onehot, axis=1)
    target = entries * MOST + slot_index
    entry_rows = jnp.arange(entries.shape[0], dtype=jnp.int32) // top_count
    source_row = jnp.zeros((EXPERTS * MOST,), jnp.int32).at[target].set(entry_rows)
    filled = jnp.zeros((EXPERTS * MOST,), jnp.bool_).at[target].set(True)
    outgoing = jnp.where(filled[:, None], normed[source_row], jnp.zeros((), jnp.bfloat16)).reshape(
        EXPERTS, MOST, width
    )
    arrived = lax.all_to_all(outgoing, "ex", split_axis=0, concat_axis=0, tiled=True).reshape(
        groups * MOST, width
    )
    arrived_rows = lax.all_gather(arrived, "sh", axis=0, tiled=True)
    gate_value = jnp.dot(arrived_rows, gate_weight[0], preferred_element_type=jnp.float32)
    up_value = jnp.dot(arrived_rows, up_weight[0], preferred_element_type=jnp.float32)
    hidden = (jax.nn.silu(gate_value) * up_value).astype(jnp.bfloat16)
    partial = jnp.dot(hidden, down_weight[0], preferred_element_type=jnp.float32).astype(jnp.bfloat16)
    summed = lax.psum_scatter(partial, "sh", scatter_dimension=0, tiled=True)
    returned = lax.all_to_all(
        summed.reshape(EXPERTS, MOST, width), "ex", split_axis=0, concat_axis=0, tiled=True
    )
    flat_results = returned.reshape(EXPERTS * MOST, width)
    picked = flat_results[target].reshape(row_count, top_count, width)
    mixed = resid + jnp.sum(route_weights[:, :, None] * picked.astype(jnp.float32), axis=1)
    return rms_scale(mixed, out_gain).astype(jnp.bfloat16)


def solution(mesh):
    placed = (
        P(("ex", "sh"), None),
        P(("ex", "sh"), None),
        P(("ex", "sh"), None),
        P(("ex", "sh"), None),
        P(("ex", "sh"), None),
        P(("ex", "sh"), None),
        P(("ex", "sh"), None),
        P(("ex", "sh"), None),
        P(("ex", "sh"), None),
        P(("ex", "sh"), None),
        P(),
        P(),
        P("ex", None, "sh"),
        P("ex", None, "sh"),
        P("ex", "sh", None),
        P(),
    )
    return jax.shard_map(
        per_device, mesh=mesh, in_specs=placed, out_specs=P(("ex", "sh"), None), check_vma=False
    )
```

```python
import jax
import jax.numpy as jnp
from jax import lax
from jax.sharding import PartitionSpec as P

HEADS = 36
HEAD_DIM = 64
EXPERTS = 8
PAGE = 16
MOST = 32


def rms_scale(values, gain):
    mean_square = jnp.mean(values * values, axis=-1, keepdims=True)
    return values * lax.rsqrt(mean_square + 1e-05) * gain.astype(jnp.float32)


def route_probs(normed, router_weight, route_ids):
    logits = jnp.dot(normed, router_weight, preferred_element_type=jnp.float32)
    expert_range = jnp.arange(router_weight.shape[1], dtype=jnp.int32)
    picked = jnp.sum(
        jnp.where(route_ids[:, :, None] == expert_range[None, None, :], logits[:, None, :], 0.0),
        axis=2,
    )
    raised = jnp.exp(picked)
    return raised / jnp.sum(raised, axis=1, keepdims=True)


def attend(
    hidden_rows,
    query_rows,
    key_rows,
    value_rows,
    key_store,
    value_store,
    page_row,
    new_row_lengths,
    context_row_lengths,
):
    row_count = query_rows.shape[0]
    store_count = key_store.shape[0]
    requests = new_row_lengths.shape[0]
    table = page_row.reshape(requests, -1)
    per_request = table.shape[1]
    ends = jnp.cumsum(new_row_lengths)
    row_index = jnp.arange(row_count, dtype=jnp.int32)
    owner = jnp.sum((row_index[:, None] >= ends[None, :]).astype(jnp.int32), axis=1)
    request_index = jnp.arange(requests, dtype=jnp.int32)
    row_owner = owner[:, None] == request_index[None, :]
    token_index = jnp.arange(store_count, dtype=jnp.int32)
    token_page = token_index // PAGE
    token_offset = token_index % PAGE
    matched = table[:, :, None] == token_page[None, None, :]
    page_slot = jnp.arange(per_request, dtype=jnp.int32) * PAGE
    position = (
        jnp.sum(jnp.where(matched, page_slot[None, :, None], 0), axis=1) + token_offset[None, :]
    )
    visible = jnp.any(matched, axis=1) & (position < context_row_lengths[:, None])
    store_mask = jnp.any(row_owner[:, :, None] & visible[None, :, :], axis=1)
    fresh_mask = (owner[:, None] == owner[None, :]) & (row_index[None, :] <= row_index[:, None])
    allowed = jnp.concatenate([store_mask, fresh_mask], axis=1)
    keys = jnp.concatenate([key_store, key_rows], axis=0).reshape(-1, HEADS, HEAD_DIM)
    values = jnp.concatenate([value_store, value_rows], axis=0).reshape(-1, HEADS, HEAD_DIM)
    query_heads = query_rows.reshape(row_count, HEADS, HEAD_DIM)
    scores = jnp.einsum(
        "rhd,khd->hrk", query_heads, keys, preferred_element_type=jnp.float32
    ) * HEAD_DIM ** (-0.5)
    raised = jnp.where(allowed[None, :, :], jnp.exp(scores), 0.0)
    weights = (raised / jnp.sum(raised, axis=2, keepdims=True)).astype(jnp.bfloat16)
    attended = jnp.einsum(
        "hrk,khd->rhd", weights, values, preferred_element_type=jnp.float32
    ).reshape(row_count, HEADS * HEAD_DIM)
    return hidden_rows.astype(jnp.float32) + attended


def per_device(
    hidden_in,
    queries,
    new_keys,
    new_values,
    key_pool,
    value_pool,
    page_order,
    new_lengths,
    context_lengths,
    route_ids,
    norm_gain,
    router_weight,
    gate_weight,
    up_weight,
    down_weight,
    out_gain,
):
    groups = lax.axis_size("ex")
    local_experts = gate_weight.shape[0]
    width = hidden_in.shape[1]
    row_count = hidden_in.shape[0]
    resid = attend(
        hidden_in,
        queries,
        new_keys,
        new_values,
        key_pool,
        value_pool,
        page_order[0],
        new_lengths[0],
        context_lengths[0],
    )
    normed = rms_scale(resid, norm_gain).astype(jnp.bfloat16)
    route_weights = route_probs(normed, router_weight, route_ids)
    top_count = route_ids.shape[1]
    entries = route_ids.reshape(-1)
    expert_range = jnp.arange(EXPERTS, dtype=jnp.int32)
    onehot = (entries[:, None] == expert_range[None, :]).astype(jnp.int32)
    before = jnp.cumsum(onehot, axis=0) - onehot
    slot_index = jnp.sum(before * onehot, axis=1)
    target = entries * MOST + slot_index
    entry_rows = jnp.arange(entries.shape[0], dtype=jnp.int32) // top_count
    source_row = jnp.zeros((EXPERTS * MOST,), jnp.int32).at[target].set(entry_rows)
    filled = jnp.zeros((EXPERTS * MOST,), jnp.bool_).at[target].set(True)
    outgoing = jnp.where(filled[:, None], normed[source_row], jnp.zeros((), jnp.bfloat16)).reshape(
        EXPERTS, MOST, width
    )
    cuts = 3
    step = width // cuts
    gate_value = 0.0
    up_value = 0.0
    for cut in range(cuts):
        columns = slice(cut * step, (cut + 1) * step)
        arrived = lax.all_to_all(
            outgoing[:, :, columns], "ex", split_axis=0, concat_axis=0, tiled=True
        ).reshape(groups * MOST, step)
        arrived_rows = lax.all_gather(arrived, "sh", axis=0, tiled=True)
        gate_value = gate_value + jnp.dot(
            arrived_rows, gate_weight[0, columns], preferred_element_type=jnp.float32
        )
        up_value = up_value + jnp.dot(
            arrived_rows, up_weight[0, columns], preferred_element_type=jnp.float32
        )
    hidden = (jax.nn.silu(gate_value) * up_value).astype(jnp.bfloat16)
    pieces = []
    for cut in range(cuts):
        columns = slice(cut * step, (cut + 1) * step)
        partial = jnp.dot(
            hidden, down_weight[0, :, columns], preferred_element_type=jnp.float32
        ).astype(jnp.bfloat16)
        summed = lax.psum_scatter(partial, "sh", scatter_dimension=0, tiled=True)
        pieces.append(
            lax.all_to_all(
                summed.reshape(EXPERTS, MOST, step), "ex", split_axis=0, concat_axis=0, tiled=True
            )
        )
    returned = jnp.concatenate(pieces, axis=2)
    flat_results = returned.reshape(EXPERTS * MOST, width)
    picked = flat_results[target].reshape(row_count, top_count, width)
    mixed = resid + jnp.sum(route_weights[:, :, None] * picked.astype(jnp.float32), axis=1)
    return rms_scale(mixed, out_gain).astype(jnp.bfloat16)


def solution(mesh):
    placed = (
        P(("ex", "sh"), None),
        P(("ex", "sh"), None),
        P(("ex", "sh"), None),
        P(("ex", "sh"), None),
        P(("ex", "sh"), None),
        P(("ex", "sh"), None),
        P(("ex", "sh"), None),
        P(("ex", "sh"), None),
        P(("ex", "sh"), None),
        P(("ex", "sh"), None),
        P(),
        P(),
        P("ex", None, "sh"),
        P("ex", None, "sh"),
        P("ex", "sh", None),
        P(),
    )
    return jax.shard_map(
        per_device, mesh=mesh, in_specs=placed, out_specs=P(("ex", "sh"), None), check_vma=False
    )
```

```python
import jax
import jax.numpy as jnp
from jax import lax
from jax.sharding import PartitionSpec as P

HEADS = 36
HEAD_DIM = 64
EXPERTS = 8
PAGE = 16
MOST = 32
CTX_TOTAL = 512


def rms_scale(values, gain):
    mean_square = jnp.mean(values * values, axis=-1, keepdims=True)
    return values * lax.rsqrt(mean_square + 1e-05) * gain.astype(jnp.float32)


def route_probs(normed, router_weight, route_ids):
    logits = jnp.dot(normed, router_weight, preferred_element_type=jnp.float32)
    expert_range = jnp.arange(router_weight.shape[1], dtype=jnp.int32)
    picked = jnp.sum(
        jnp.where(route_ids[:, :, None] == expert_range[None, None, :], logits[:, None, :], 0.0),
        axis=2,
    )
    raised = jnp.exp(picked)
    return raised / jnp.sum(raised, axis=1, keepdims=True)


def attend(
    hidden_rows,
    query_rows,
    key_rows,
    value_rows,
    key_store,
    value_store,
    page_row,
    new_row_lengths,
    context_row_lengths,
):
    row_count = query_rows.shape[0]
    requests = new_row_lengths.shape[0]
    table = page_row.reshape(requests, -1)
    ends = jnp.cumsum(new_row_lengths)
    row_index = jnp.arange(row_count, dtype=jnp.int32)
    owner = jnp.sum((row_index[:, None] >= ends[None, :]).astype(jnp.int32), axis=1)
    context_ends = jnp.cumsum(context_row_lengths)
    slot = jnp.arange(CTX_TOTAL, dtype=jnp.int32)
    slot_owner = jnp.sum((slot[:, None] >= context_ends[None, :]).astype(jnp.int32), axis=1)
    position = slot - (context_ends - context_row_lengths)[slot_owner]
    token = table[slot_owner, position // PAGE] * PAGE + position % PAGE
    key_store = key_store[token]
    value_store = value_store[token]
    store_mask = owner[:, None] == slot_owner[None, :]
    fresh_mask = (owner[:, None] == owner[None, :]) & (row_index[None, :] <= row_index[:, None])
    allowed = jnp.concatenate([store_mask, fresh_mask], axis=1)
    keys = jnp.concatenate([key_store, key_rows], axis=0).reshape(-1, HEADS, HEAD_DIM)
    values = jnp.concatenate([value_store, value_rows], axis=0).reshape(-1, HEADS, HEAD_DIM)
    query_heads = query_rows.reshape(row_count, HEADS, HEAD_DIM)
    scores = jnp.einsum(
        "rhd,khd->hrk", query_heads, keys, preferred_element_type=jnp.float32
    ) * HEAD_DIM ** (-0.5)
    raised = jnp.where(allowed[None, :, :], jnp.exp(scores), 0.0)
    weights = (raised / jnp.sum(raised, axis=2, keepdims=True)).astype(jnp.bfloat16)
    attended = jnp.einsum(
        "hrk,khd->rhd", weights, values, preferred_element_type=jnp.float32
    ).reshape(row_count, HEADS * HEAD_DIM)
    return hidden_rows.astype(jnp.float32) + attended


def per_device(
    hidden_in,
    queries,
    new_keys,
    new_values,
    key_pool,
    value_pool,
    page_order,
    new_lengths,
    context_lengths,
    route_ids,
    norm_gain,
    router_weight,
    gate_weight,
    up_weight,
    down_weight,
    out_gain,
):
    groups = lax.axis_size("ex")
    local_experts = gate_weight.shape[0]
    width = hidden_in.shape[1]
    row_count = hidden_in.shape[0]
    resid = attend(
        hidden_in,
        queries,
        new_keys,
        new_values,
        key_pool,
        value_pool,
        page_order[0],
        new_lengths[0],
        context_lengths[0],
    )
    normed = rms_scale(resid, norm_gain).astype(jnp.bfloat16)
    route_weights = route_probs(normed, router_weight, route_ids)
    top_count = route_ids.shape[1]
    entries = route_ids.reshape(-1)
    expert_range = jnp.arange(EXPERTS, dtype=jnp.int32)
    onehot = (entries[:, None] == expert_range[None, :]).astype(jnp.int32)
    before = jnp.cumsum(onehot, axis=0) - onehot
    slot_index = jnp.sum(before * onehot, axis=1)
    target = entries * MOST + slot_index
    entry_rows = jnp.arange(entries.shape[0], dtype=jnp.int32) // top_count
    source_row = jnp.zeros((EXPERTS * MOST,), jnp.int32).at[target].set(entry_rows)
    filled = jnp.zeros((EXPERTS * MOST,), jnp.bool_).at[target].set(True)
    outgoing = jnp.where(filled[:, None], normed[source_row], jnp.zeros((), jnp.bfloat16)).reshape(
        EXPERTS, MOST, width
    )
    arrived = lax.all_to_all(outgoing, "ex", split_axis=0, concat_axis=0, tiled=True).reshape(
        groups * MOST, width
    )
    arrived_rows = lax.all_gather(arrived, "sh", axis=0, tiled=True)
    gate_value = jnp.dot(arrived_rows, gate_weight[0], preferred_element_type=jnp.float32)
    up_value = jnp.dot(arrived_rows, up_weight[0], preferred_element_type=jnp.float32)
    hidden = (jax.nn.silu(gate_value) * up_value).astype(jnp.bfloat16)
    partial = jnp.dot(hidden, down_weight[0], preferred_element_type=jnp.float32).astype(jnp.bfloat16)
    summed = lax.psum_scatter(partial, "sh", scatter_dimension=0, tiled=True)
    returned = lax.all_to_all(
        summed.reshape(EXPERTS, MOST, width), "ex", split_axis=0, concat_axis=0, tiled=True
    )
    flat_results = returned.reshape(EXPERTS * MOST, width)
    picked = flat_results[target].reshape(row_count, top_count, width)
    mixed = resid + jnp.sum(route_weights[:, :, None] * picked.astype(jnp.float32), axis=1)
    return rms_scale(mixed, out_gain).astype(jnp.bfloat16)


def solution(mesh):
    placed = (
        P(("ex", "sh"), None),
        P(("ex", "sh"), None),
        P(("ex", "sh"), None),
        P(("ex", "sh"), None),
        P(("ex", "sh"), None),
        P(("ex", "sh"), None),
        P(("ex", "sh"), None),
        P(("ex", "sh"), None),
        P(("ex", "sh"), None),
        P(("ex", "sh"), None),
        P(),
        P(),
        P("ex", None, "sh"),
        P("ex", None, "sh"),
        P("ex", "sh", None),
        P(),
    )
    return jax.shard_map(
        per_device, mesh=mesh, in_specs=placed, out_specs=P(("ex", "sh"), None), check_vma=False
    )
```

```python
import jax
import jax.numpy as jnp
from jax import lax
from jax.sharding import PartitionSpec as P
from jax.experimental import pallas as pl

HEADS = 36
HEAD_DIM = 64
EXPERTS = 8
PAGE = 16
MOST = 32
INTERPRET = False


def rms_scale(values, gain):
    mean_square = jnp.mean(values * values, axis=-1, keepdims=True)
    return values * lax.rsqrt(mean_square + 1e-05) * gain.astype(jnp.float32)


def route_probs(normed, router_weight, route_ids):
    logits = jnp.dot(normed, router_weight, preferred_element_type=jnp.float32)
    expert_range = jnp.arange(router_weight.shape[1], dtype=jnp.int32)
    picked = jnp.sum(
        jnp.where(route_ids[:, :, None] == expert_range[None, None, :], logits[:, None, :], 0.0),
        axis=2,
    )
    raised = jnp.exp(picked)
    return raised / jnp.sum(raised, axis=1, keepdims=True)


def attention_kernel(
    query_ref, pool_key_ref, new_key_ref, pool_value_ref, new_value_ref, hidden_ref,
    token_owner_ref, owner_ref, owner_row_ref, out_ref
):
    query = query_ref[...]
    rows = query.shape[0]
    owner = owner_ref[...]
    pool_ok = owner == token_owner_ref[...]
    row_at = lax.broadcasted_iota(jnp.int32, (rows, rows), 0)
    col_at = lax.broadcasted_iota(jnp.int32, (rows, rows), 1)
    new_ok = (owner == owner_row_ref[...]) & (col_at <= row_at)
    lane = lax.broadcasted_iota(jnp.int32, (1, query.shape[1]), 1)
    contract = (((1,), (1,)), ((), ()))
    total = hidden_ref[...].astype(jnp.float32)
    for head in range(query.shape[1] // HEAD_DIM):
        in_head = (lane >= head * HEAD_DIM) & (lane < (head + 1) * HEAD_DIM)
        head_query = jnp.where(in_head, query, jnp.zeros((), query.dtype))
        pool_score = lax.dot_general(
            head_query, pool_key_ref[...], contract, preferred_element_type=jnp.float32
        ) * HEAD_DIM ** (-0.5)
        new_score = lax.dot_general(
            head_query, new_key_ref[...], contract, preferred_element_type=jnp.float32
        ) * HEAD_DIM ** (-0.5)
        pool_raised = jnp.where(pool_ok, jnp.exp(pool_score), 0.0)
        new_raised = jnp.where(new_ok, jnp.exp(new_score), 0.0)
        denom = jnp.sum(pool_raised, axis=1, keepdims=True) + jnp.sum(
            new_raised, axis=1, keepdims=True
        )
        pool_weight = (pool_raised / denom).astype(jnp.bfloat16)
        new_weight = (new_raised / denom).astype(jnp.bfloat16)
        mixed = jnp.dot(
            pool_weight, pool_value_ref[...], preferred_element_type=jnp.float32
        ) + jnp.dot(new_weight, new_value_ref[...], preferred_element_type=jnp.float32)
        total = total + jnp.where(in_head, mixed, 0.0)
    out_ref[...] = total


def attend(
    hidden_rows,
    query_rows,
    key_rows,
    value_rows,
    key_store,
    value_store,
    page_row,
    new_row_lengths,
    context_row_lengths,
):
    row_count, width = query_rows.shape
    store_count = key_store.shape[0]
    requests = new_row_lengths.shape[0]
    per_request = page_row.shape[0] // requests
    ends = jnp.cumsum(new_row_lengths)
    row_index = jnp.arange(row_count, dtype=jnp.int32)
    owner = jnp.sum((row_index[:, None] >= ends[None, :]).astype(jnp.int32), axis=1)
    pages = store_count // PAGE
    entry = jnp.arange(page_row.shape[0], dtype=jnp.int32)
    page_entry = jnp.sum(
        jnp.where(page_row[None, :] == jnp.arange(pages, dtype=jnp.int32)[:, None], entry[None, :], 0),
        axis=1,
    )
    token_index = jnp.arange(store_count, dtype=jnp.int32)
    token_entry = page_entry[token_index // PAGE]
    token_request = token_entry // per_request
    position = (token_entry % per_request) * PAGE + token_index % PAGE
    token_owner = jnp.where(
        position < context_row_lengths[token_request], token_request, -1
    ).astype(jnp.int32)
    block = 2 * HEAD_DIM
    column = lambda count: pl.BlockSpec((count, block), lambda j: (0, j))
    whole = lambda shape: pl.BlockSpec(shape, lambda j: (0, 0))
    return pl.pallas_call(
        attention_kernel,
        grid=(width // block,),
        in_specs=[
            column(row_count),
            column(store_count),
            column(row_count),
            column(store_count),
            column(row_count),
            column(row_count),
            whole((1, store_count)),
            whole((row_count, 1)),
            whole((1, row_count)),
        ],
        out_specs=column(row_count),
        out_shape=jax.ShapeDtypeStruct((row_count, width), jnp.float32),
        interpret=INTERPRET,
    )(
        query_rows,
        key_store,
        key_rows,
        value_store,
        value_rows,
        hidden_rows,
        token_owner.reshape(1, store_count),
        owner.reshape(row_count, 1),
        owner.reshape(1, row_count),
    )


def per_device(
    hidden_in,
    queries,
    new_keys,
    new_values,
    key_pool,
    value_pool,
    page_order,
    new_lengths,
    context_lengths,
    route_ids,
    norm_gain,
    router_weight,
    gate_weight,
    up_weight,
    down_weight,
    out_gain,
):
    groups = lax.axis_size("ex")
    local_experts = gate_weight.shape[0]
    width = hidden_in.shape[1]
    row_count = hidden_in.shape[0]
    resid = attend(
        hidden_in,
        queries,
        new_keys,
        new_values,
        key_pool,
        value_pool,
        page_order[0],
        new_lengths[0],
        context_lengths[0],
    )
    normed = rms_scale(resid, norm_gain).astype(jnp.bfloat16)
    route_weights = route_probs(normed, router_weight, route_ids)
    top_count = route_ids.shape[1]
    entries = route_ids.reshape(-1)
    expert_range = jnp.arange(EXPERTS, dtype=jnp.int32)
    onehot = (entries[:, None] == expert_range[None, :]).astype(jnp.int32)
    before = jnp.cumsum(onehot, axis=0) - onehot
    slot_index = jnp.sum(before * onehot, axis=1)
    target = entries * MOST + slot_index
    entry_rows = jnp.arange(entries.shape[0], dtype=jnp.int32) // top_count
    source_row = jnp.zeros((EXPERTS * MOST,), jnp.int32).at[target].set(entry_rows)
    filled = jnp.zeros((EXPERTS * MOST,), jnp.bool_).at[target].set(True)
    outgoing = jnp.where(filled[:, None], normed[source_row], jnp.zeros((), jnp.bfloat16)).reshape(
        EXPERTS, MOST, width
    )
    arrived = lax.all_to_all(outgoing, "ex", split_axis=0, concat_axis=0, tiled=True).reshape(
        groups * MOST, width
    )
    arrived_rows = lax.all_gather(arrived, "sh", axis=0, tiled=True)
    gate_value = jnp.dot(arrived_rows, gate_weight[0], preferred_element_type=jnp.float32)
    up_value = jnp.dot(arrived_rows, up_weight[0], preferred_element_type=jnp.float32)
    hidden = (jax.nn.silu(gate_value) * up_value).astype(jnp.bfloat16)
    partial = jnp.dot(hidden, down_weight[0], preferred_element_type=jnp.float32).astype(jnp.bfloat16)
    summed = lax.psum_scatter(partial, "sh", scatter_dimension=0, tiled=True)
    returned = lax.all_to_all(
        summed.reshape(EXPERTS, MOST, width), "ex", split_axis=0, concat_axis=0, tiled=True
    )
    flat_results = returned.reshape(EXPERTS * MOST, width)
    picked = flat_results[target].reshape(row_count, top_count, width)
    mixed = resid + jnp.sum(route_weights[:, :, None] * picked.astype(jnp.float32), axis=1)
    return rms_scale(mixed, out_gain).astype(jnp.bfloat16)


def solution(mesh):
    placed = (
        P(("ex", "sh"), None),
        P(("ex", "sh"), None),
        P(("ex", "sh"), None),
        P(("ex", "sh"), None),
        P(("ex", "sh"), None),
        P(("ex", "sh"), None),
        P(("ex", "sh"), None),
        P(("ex", "sh"), None),
        P(("ex", "sh"), None),
        P(("ex", "sh"), None),
        P(),
        P(),
        P("ex", None, "sh"),
        P("ex", None, "sh"),
        P("ex", "sh", None),
        P(),
    )
    return jax.shard_map(
        per_device, mesh=mesh, in_specs=placed, out_specs=P(("ex", "sh"), None), check_vma=False
    )
```

```python
import jax
import jax.numpy as jnp
from jax import lax
from jax.sharding import PartitionSpec as P
from jax.experimental import pallas as pl

HEADS = 36
HEAD_DIM = 64
EXPERTS = 8
PAGE = 16
MOST = 32
INTERPRET = False


def rms_scale(values, gain):
    mean_square = jnp.mean(values * values, axis=-1, keepdims=True)
    return values * lax.rsqrt(mean_square + 1e-05) * gain.astype(jnp.float32)


def route_probs(normed, router_weight, route_ids):
    logits = jnp.dot(normed, router_weight, preferred_element_type=jnp.float32)
    expert_range = jnp.arange(router_weight.shape[1], dtype=jnp.int32)
    picked = jnp.sum(
        jnp.where(route_ids[:, :, None] == expert_range[None, None, :], logits[:, None, :], 0.0),
        axis=2,
    )
    raised = jnp.exp(picked)
    return raised / jnp.sum(raised, axis=1, keepdims=True)


def attention_kernel(
    query_ref, pool_key_ref, new_key_ref, pool_value_ref, new_value_ref, hidden_ref,
    token_owner_ref, owner_ref, owner_row_ref, out_ref
):
    query = query_ref[...]
    rows = query.shape[0]
    owner = owner_ref[...]
    pool_ok = owner == token_owner_ref[...]
    row_at = lax.broadcasted_iota(jnp.int32, (rows, rows), 0)
    col_at = lax.broadcasted_iota(jnp.int32, (rows, rows), 1)
    new_ok = (owner == owner_row_ref[...]) & (col_at <= row_at)
    lane = lax.broadcasted_iota(jnp.int32, (1, query.shape[1]), 1)
    contract = (((1,), (1,)), ((), ()))
    total = hidden_ref[...].astype(jnp.float32)
    for head in range(query.shape[1] // HEAD_DIM):
        in_head = (lane >= head * HEAD_DIM) & (lane < (head + 1) * HEAD_DIM)
        head_query = jnp.where(in_head, query, jnp.zeros((), query.dtype))
        pool_score = lax.dot_general(
            head_query, pool_key_ref[...], contract, preferred_element_type=jnp.float32
        ) * HEAD_DIM ** (-0.5)
        new_score = lax.dot_general(
            head_query, new_key_ref[...], contract, preferred_element_type=jnp.float32
        ) * HEAD_DIM ** (-0.5)
        pool_raised = jnp.where(pool_ok, jnp.exp(pool_score), 0.0)
        new_raised = jnp.where(new_ok, jnp.exp(new_score), 0.0)
        denom = jnp.sum(pool_raised, axis=1, keepdims=True) + jnp.sum(
            new_raised, axis=1, keepdims=True
        )
        pool_weight = (pool_raised / denom).astype(jnp.bfloat16)
        new_weight = (new_raised / denom).astype(jnp.bfloat16)
        mixed = jnp.dot(
            pool_weight, pool_value_ref[...], preferred_element_type=jnp.float32
        ) + jnp.dot(new_weight, new_value_ref[...], preferred_element_type=jnp.float32)
        total = total + jnp.where(in_head, mixed, 0.0)
    out_ref[...] = total


def attend(
    hidden_rows,
    query_rows,
    key_rows,
    value_rows,
    key_store,
    value_store,
    page_row,
    new_row_lengths,
    context_row_lengths,
):
    row_count, width = query_rows.shape
    store_count = key_store.shape[0]
    requests = new_row_lengths.shape[0]
    per_request = page_row.shape[0] // requests
    ends = jnp.cumsum(new_row_lengths)
    row_index = jnp.arange(row_count, dtype=jnp.int32)
    owner = jnp.sum((row_index[:, None] >= ends[None, :]).astype(jnp.int32), axis=1)
    entry = jnp.arange(page_row.shape[0], dtype=jnp.int32)
    token_index = jnp.arange(store_count, dtype=jnp.int32)
    hit = page_row[:, None] == (token_index // PAGE)[None, :]
    token_entry = jnp.sum(jnp.where(hit, entry[:, None], 0), axis=0)
    token_request = token_entry // per_request
    position = (token_entry % per_request) * PAGE + token_index % PAGE
    request_index = jnp.arange(requests, dtype=jnp.int32)
    limit = jnp.sum(
        jnp.where(
            token_request[None, :] == request_index[:, None], context_row_lengths[:, None], 0
        ),
        axis=0,
    )
    token_owner = jnp.where(position < limit, token_request, -1).astype(jnp.int32)
    block = 2 * HEAD_DIM
    column = lambda count: pl.BlockSpec((count, block), lambda j: (0, j))
    whole = lambda shape: pl.BlockSpec(shape, lambda j: (0, 0))
    return pl.pallas_call(
        attention_kernel,
        grid=(width // block,),
        in_specs=[
            column(row_count),
            column(store_count),
            column(row_count),
            column(store_count),
            column(row_count),
            column(row_count),
            whole((1, store_count)),
            whole((row_count, 1)),
            whole((1, row_count)),
        ],
        out_specs=column(row_count),
        out_shape=jax.ShapeDtypeStruct((row_count, width), jnp.float32),
        interpret=INTERPRET,
    )(
        query_rows,
        key_store,
        key_rows,
        value_store,
        value_rows,
        hidden_rows,
        token_owner.reshape(1, store_count),
        owner.reshape(row_count, 1),
        owner.reshape(1, row_count),
    )


def per_device(
    hidden_in,
    queries,
    new_keys,
    new_values,
    key_pool,
    value_pool,
    page_order,
    new_lengths,
    context_lengths,
    route_ids,
    norm_gain,
    router_weight,
    gate_weight,
    up_weight,
    down_weight,
    out_gain,
):
    groups = lax.axis_size("ex")
    local_experts = gate_weight.shape[0]
    width = hidden_in.shape[1]
    row_count = hidden_in.shape[0]
    resid = attend(
        hidden_in,
        queries,
        new_keys,
        new_values,
        key_pool,
        value_pool,
        page_order[0],
        new_lengths[0],
        context_lengths[0],
    )
    normed = rms_scale(resid, norm_gain).astype(jnp.bfloat16)
    route_weights = route_probs(normed, router_weight, route_ids)
    top_count = route_ids.shape[1]
    entries = route_ids.reshape(-1)
    expert_range = jnp.arange(EXPERTS, dtype=jnp.int32)
    onehot = (entries[:, None] == expert_range[None, :]).astype(jnp.int32)
    before = jnp.cumsum(onehot, axis=0) - onehot
    slot_index = jnp.sum(before * onehot, axis=1)
    target = entries * MOST + slot_index
    entry_rows = jnp.arange(entries.shape[0], dtype=jnp.int32) // top_count
    source_row = jnp.zeros((EXPERTS * MOST,), jnp.int32).at[target].set(entry_rows)
    filled = jnp.zeros((EXPERTS * MOST,), jnp.bool_).at[target].set(True)
    outgoing = jnp.where(filled[:, None], normed[source_row], jnp.zeros((), jnp.bfloat16)).reshape(
        EXPERTS, MOST, width
    )
    arrived = lax.all_to_all(outgoing, "ex", split_axis=0, concat_axis=0, tiled=True).reshape(
        groups * MOST, width
    )
    arrived_rows = lax.all_gather(arrived, "sh", axis=0, tiled=True)
    gate_value = jnp.dot(arrived_rows, gate_weight[0], preferred_element_type=jnp.float32)
    up_value = jnp.dot(arrived_rows, up_weight[0], preferred_element_type=jnp.float32)
    hidden = (jax.nn.silu(gate_value) * up_value).astype(jnp.bfloat16)
    partial = jnp.dot(hidden, down_weight[0], preferred_element_type=jnp.float32).astype(jnp.bfloat16)
    summed = lax.psum_scatter(partial, "sh", scatter_dimension=0, tiled=True)
    returned = lax.all_to_all(
        summed.reshape(EXPERTS, MOST, width), "ex", split_axis=0, concat_axis=0, tiled=True
    )
    flat_results = returned.reshape(EXPERTS * MOST, width)
    picked = flat_results[target].reshape(row_count, top_count, width)
    mixed = resid + jnp.sum(route_weights[:, :, None] * picked.astype(jnp.float32), axis=1)
    return rms_scale(mixed, out_gain).astype(jnp.bfloat16)


def solution(mesh):
    placed = (
        P(("ex", "sh"), None),
        P(("ex", "sh"), None),
        P(("ex", "sh"), None),
        P(("ex", "sh"), None),
        P(("ex", "sh"), None),
        P(("ex", "sh"), None),
        P(("ex", "sh"), None),
        P(("ex", "sh"), None),
        P(("ex", "sh"), None),
        P(("ex", "sh"), None),
        P(),
        P(),
        P("ex", None, "sh"),
        P("ex", None, "sh"),
        P("ex", "sh", None),
        P(),
    )
    return jax.shard_map(
        per_device, mesh=mesh, in_specs=placed, out_specs=P(("ex", "sh"), None), check_vma=False
    )
```

```python
import jax
import jax.numpy as jnp
from jax import lax
from jax.sharding import PartitionSpec as P
from jax.experimental import pallas as pl

HEADS = 36
HEAD_DIM = 64
EXPERTS = 8
PAGE = 16
MOST = 32
INTERPRET = False


def rms_scale(values, gain):
    mean_square = jnp.mean(values * values, axis=-1, keepdims=True)
    return values * lax.rsqrt(mean_square + 1e-05) * gain.astype(jnp.float32)


def route_probs(normed, router_weight, route_ids):
    logits = jnp.dot(normed, router_weight, preferred_element_type=jnp.float32)
    expert_range = jnp.arange(router_weight.shape[1], dtype=jnp.int32)
    picked = jnp.sum(
        jnp.where(route_ids[:, :, None] == expert_range[None, None, :], logits[:, None, :], 0.0),
        axis=2,
    )
    raised = jnp.exp(picked)
    return raised / jnp.sum(raised, axis=1, keepdims=True)


def attention_kernel(
    query_ref, pool_key_ref, new_key_ref, pool_value_ref, new_value_ref, hidden_ref,
    token_owner_ref, owner_ref, owner_row_ref, out_ref
):
    query = query_ref[...]
    rows = query.shape[0]
    owner = owner_ref[...]
    pool_ok = owner == token_owner_ref[...]
    row_at = lax.broadcasted_iota(jnp.int32, (rows, rows), 0)
    col_at = lax.broadcasted_iota(jnp.int32, (rows, rows), 1)
    new_ok = (owner == owner_row_ref[...]) & (col_at <= row_at)
    lane = lax.broadcasted_iota(jnp.int32, (1, query.shape[1]), 1)
    contract = (((1,), (1,)), ((), ()))
    total = hidden_ref[...].astype(jnp.float32)
    for head in range(query.shape[1] // HEAD_DIM):
        in_head = (lane >= head * HEAD_DIM) & (lane < (head + 1) * HEAD_DIM)
        head_query = jnp.where(in_head, query, jnp.zeros((), query.dtype))
        pool_score = lax.dot_general(
            head_query, pool_key_ref[...], contract, preferred_element_type=jnp.float32
        ) * HEAD_DIM ** (-0.5)
        new_score = lax.dot_general(
            head_query, new_key_ref[...], contract, preferred_element_type=jnp.float32
        ) * HEAD_DIM ** (-0.5)
        pool_raised = jnp.where(pool_ok, jnp.exp(pool_score), 0.0)
        new_raised = jnp.where(new_ok, jnp.exp(new_score), 0.0)
        denom = jnp.sum(pool_raised, axis=1, keepdims=True) + jnp.sum(
            new_raised, axis=1, keepdims=True
        )
        pool_weight = (pool_raised / denom).astype(jnp.bfloat16)
        new_weight = (new_raised / denom).astype(jnp.bfloat16)
        mixed = jnp.dot(
            pool_weight, pool_value_ref[...], preferred_element_type=jnp.float32
        ) + jnp.dot(new_weight, new_value_ref[...], preferred_element_type=jnp.float32)
        total = total + jnp.where(in_head, mixed, 0.0)
    out_ref[...] = total


def attend(
    hidden_rows,
    query_rows,
    key_rows,
    value_rows,
    key_store,
    value_store,
    page_row,
    new_row_lengths,
    context_row_lengths,
):
    row_count, width = query_rows.shape
    store_count = key_store.shape[0]
    requests = new_row_lengths.shape[0]
    per_request = page_row.shape[0] // requests
    ends = jnp.cumsum(new_row_lengths)
    row_index = jnp.arange(row_count, dtype=jnp.int32)
    owner = jnp.sum((row_index[:, None] >= ends[None, :]).astype(jnp.int32), axis=1)
    entry = jnp.arange(page_row.shape[0], dtype=jnp.int32)
    token_index = jnp.arange(store_count, dtype=jnp.int32)
    hit = page_row[:, None] == (token_index // PAGE)[None, :]
    token_entry = jnp.sum(jnp.where(hit, entry[:, None], 0), axis=0)
    token_request = token_entry // per_request
    position = (token_entry % per_request) * PAGE + token_index % PAGE
    request_index = jnp.arange(requests, dtype=jnp.int32)
    limit = jnp.sum(
        jnp.where(
            token_request[None, :] == request_index[:, None], context_row_lengths[:, None], 0
        ),
        axis=0,
    )
    token_owner = jnp.where(position < limit, token_request, -1).astype(jnp.int32)
    block = 2 * HEAD_DIM
    column = lambda count: pl.BlockSpec((count, block), lambda j: (0, j))
    whole = lambda shape: pl.BlockSpec(shape, lambda j: (0, 0))
    return pl.pallas_call(
        attention_kernel,
        grid=(width // block,),
        in_specs=[
            column(row_count),
            column(store_count),
            column(row_count),
            column(store_count),
            column(row_count),
            column(row_count),
            whole((1, store_count)),
            whole((row_count, 1)),
            whole((1, row_count)),
        ],
        out_specs=column(row_count),
        out_shape=jax.ShapeDtypeStruct((row_count, width), jnp.float32),
        interpret=INTERPRET,
    )(
        query_rows,
        key_store,
        key_rows,
        value_store,
        value_rows,
        hidden_rows,
        token_owner.reshape(1, store_count),
        owner.reshape(row_count, 1),
        owner.reshape(1, row_count),
    )


def ffn_kernel(rows_ref, gate_ref, up_ref, down_ref, out_ref):
    rows = rows_ref[...]
    gate_value = jnp.dot(rows, gate_ref[...], preferred_element_type=jnp.float32)
    up_value = jnp.dot(rows, up_ref[...], preferred_element_type=jnp.float32)
    hidden = (gate_value / (1.0 + jnp.exp(-gate_value)) * up_value).astype(jnp.bfloat16)
    out_ref[...] = jnp.dot(hidden, down_ref[...], preferred_element_type=jnp.float32).astype(
        out_ref.dtype
    )


def expert_ffn(rows, gate, up, down):
    count, width = rows.shape
    units = gate.shape[1]
    tile = 512
    fixed = lambda shape: pl.BlockSpec(shape, lambda i: (0, 0))
    return pl.pallas_call(
        ffn_kernel,
        grid=(count // tile,),
        in_specs=[
            pl.BlockSpec((tile, width), lambda i: (i, 0)),
            fixed((width, units)),
            fixed((width, units)),
            fixed((units, width)),
        ],
        out_specs=pl.BlockSpec((tile, width), lambda i: (i, 0)),
        out_shape=jax.ShapeDtypeStruct((count, width), jnp.bfloat16),
        interpret=INTERPRET,
    )(rows, gate, up, down)


def per_device(
    hidden_in,
    queries,
    new_keys,
    new_values,
    key_pool,
    value_pool,
    page_order,
    new_lengths,
    context_lengths,
    route_ids,
    norm_gain,
    router_weight,
    gate_weight,
    up_weight,
    down_weight,
    out_gain,
):
    groups = lax.axis_size("ex")
    local_experts = gate_weight.shape[0]
    width = hidden_in.shape[1]
    row_count = hidden_in.shape[0]
    resid = attend(
        hidden_in,
        queries,
        new_keys,
        new_values,
        key_pool,
        value_pool,
        page_order[0],
        new_lengths[0],
        context_lengths[0],
    )
    normed = rms_scale(resid, norm_gain).astype(jnp.bfloat16)
    route_weights = route_probs(normed, router_weight, route_ids)
    top_count = route_ids.shape[1]
    entries = route_ids.reshape(-1)
    expert_range = jnp.arange(EXPERTS, dtype=jnp.int32)
    onehot = (entries[:, None] == expert_range[None, :]).astype(jnp.int32)
    before = jnp.cumsum(onehot, axis=0) - onehot
    slot_index = jnp.sum(before * onehot, axis=1)
    target = entries * MOST + slot_index
    entry_rows = jnp.arange(entries.shape[0], dtype=jnp.int32) // top_count
    source_row = jnp.zeros((EXPERTS * MOST,), jnp.int32).at[target].set(entry_rows)
    filled = jnp.zeros((EXPERTS * MOST,), jnp.bool_).at[target].set(True)
    outgoing = jnp.where(filled[:, None], normed[source_row], jnp.zeros((), jnp.bfloat16)).reshape(
        EXPERTS, MOST, width
    )
    arrived = lax.all_to_all(outgoing, "ex", split_axis=0, concat_axis=0, tiled=True).reshape(
        groups * MOST, width
    )
    arrived_rows = lax.all_gather(arrived, "sh", axis=0, tiled=True)
    partial = expert_ffn(arrived_rows, gate_weight[0], up_weight[0], down_weight[0])
    summed = lax.psum_scatter(partial, "sh", scatter_dimension=0, tiled=True)
    returned = lax.all_to_all(
        summed.reshape(EXPERTS, MOST, width), "ex", split_axis=0, concat_axis=0, tiled=True
    )
    flat_results = returned.reshape(EXPERTS * MOST, width)
    picked = flat_results[target].reshape(row_count, top_count, width)
    mixed = resid + jnp.sum(route_weights[:, :, None] * picked.astype(jnp.float32), axis=1)
    return rms_scale(mixed, out_gain).astype(jnp.bfloat16)


def solution(mesh):
    placed = (
        P(("ex", "sh"), None),
        P(("ex", "sh"), None),
        P(("ex", "sh"), None),
        P(("ex", "sh"), None),
        P(("ex", "sh"), None),
        P(("ex", "sh"), None),
        P(("ex", "sh"), None),
        P(("ex", "sh"), None),
        P(("ex", "sh"), None),
        P(("ex", "sh"), None),
        P(),
        P(),
        P("ex", None, "sh"),
        P("ex", None, "sh"),
        P("ex", "sh", None),
        P(),
    )
    return jax.shard_map(
        per_device, mesh=mesh, in_specs=placed, out_specs=P(("ex", "sh"), None), check_vma=False
    )
```

```python
import jax
import jax.numpy as jnp
from jax import lax
from jax.sharding import PartitionSpec as P
from jax.experimental import pallas as pl

HEADS = 36
HEAD_DIM = 64
EXPERTS = 8
PAGE = 16
MOST = 32
INTERPRET = False


def rms_scale(values, gain):
    mean_square = jnp.mean(values * values, axis=-1, keepdims=True)
    return values * lax.rsqrt(mean_square + 1e-05) * gain.astype(jnp.float32)


def route_probs(normed, router_weight, route_ids):
    logits = jnp.dot(normed, router_weight, preferred_element_type=jnp.float32)
    expert_range = jnp.arange(router_weight.shape[1], dtype=jnp.int32)
    picked = jnp.sum(
        jnp.where(route_ids[:, :, None] == expert_range[None, None, :], logits[:, None, :], 0.0),
        axis=2,
    )
    raised = jnp.exp(picked)
    return raised / jnp.sum(raised, axis=1, keepdims=True)


def attention_kernel(
    query_ref, pool_key_ref, new_key_ref, pool_value_ref, new_value_ref, hidden_ref,
    token_owner_ref, owner_ref, owner_row_ref, out_ref
):
    query = query_ref[...]
    rows = query.shape[0]
    owner = owner_ref[...]
    pool_ok = owner == token_owner_ref[...]
    row_at = lax.broadcasted_iota(jnp.int32, (rows, rows), 0)
    col_at = lax.broadcasted_iota(jnp.int32, (rows, rows), 1)
    new_ok = (owner == owner_row_ref[...]) & (col_at <= row_at)
    lane = lax.broadcasted_iota(jnp.int32, (1, query.shape[1]), 1)
    contract = (((1,), (1,)), ((), ()))
    total = hidden_ref[...].astype(jnp.float32)
    for head in range(query.shape[1] // HEAD_DIM):
        in_head = (lane >= head * HEAD_DIM) & (lane < (head + 1) * HEAD_DIM)
        head_query = jnp.where(in_head, query, jnp.zeros((), query.dtype))
        pool_score = lax.dot_general(
            head_query, pool_key_ref[...], contract, preferred_element_type=jnp.float32
        ) * HEAD_DIM ** (-0.5)
        new_score = lax.dot_general(
            head_query, new_key_ref[...], contract, preferred_element_type=jnp.float32
        ) * HEAD_DIM ** (-0.5)
        pool_raised = jnp.where(pool_ok, jnp.exp(pool_score), 0.0)
        new_raised = jnp.where(new_ok, jnp.exp(new_score), 0.0)
        denom = jnp.sum(pool_raised, axis=1, keepdims=True) + jnp.sum(
            new_raised, axis=1, keepdims=True
        )
        pool_weight = (pool_raised / denom).astype(jnp.bfloat16)
        new_weight = (new_raised / denom).astype(jnp.bfloat16)
        mixed = jnp.dot(
            pool_weight, pool_value_ref[...], preferred_element_type=jnp.float32
        ) + jnp.dot(new_weight, new_value_ref[...], preferred_element_type=jnp.float32)
        total = total + jnp.where(in_head, mixed, 0.0)
    out_ref[...] = total


def attend(
    hidden_rows,
    query_rows,
    key_rows,
    value_rows,
    key_store,
    value_store,
    page_row,
    new_row_lengths,
    context_row_lengths,
):
    row_count, width = query_rows.shape
    store_count = key_store.shape[0]
    requests = new_row_lengths.shape[0]
    per_request = page_row.shape[0] // requests
    ends = jnp.cumsum(new_row_lengths)
    row_index = jnp.arange(row_count, dtype=jnp.int32)
    owner = jnp.sum((row_index[:, None] >= ends[None, :]).astype(jnp.int32), axis=1)
    entry = jnp.arange(page_row.shape[0], dtype=jnp.int32)
    token_index = jnp.arange(store_count, dtype=jnp.int32)
    hit = page_row[:, None] == (token_index // PAGE)[None, :]
    token_entry = jnp.sum(jnp.where(hit, entry[:, None], 0), axis=0)
    token_request = token_entry // per_request
    position = (token_entry % per_request) * PAGE + token_index % PAGE
    request_index = jnp.arange(requests, dtype=jnp.int32)
    limit = jnp.sum(
        jnp.where(
            token_request[None, :] == request_index[:, None], context_row_lengths[:, None], 0
        ),
        axis=0,
    )
    token_owner = jnp.where(position < limit, token_request, -1).astype(jnp.int32)
    block = 2 * HEAD_DIM
    column = lambda count: pl.BlockSpec((count, block), lambda j: (0, j))
    whole = lambda shape: pl.BlockSpec(shape, lambda j: (0, 0))
    return pl.pallas_call(
        attention_kernel,
        grid=(width // block,),
        in_specs=[
            column(row_count),
            column(store_count),
            column(row_count),
            column(store_count),
            column(row_count),
            column(row_count),
            whole((1, store_count)),
            whole((row_count, 1)),
            whole((1, row_count)),
        ],
        out_specs=column(row_count),
        out_shape=jax.ShapeDtypeStruct((row_count, width), jnp.float32),
        interpret=INTERPRET,
    )(
        query_rows,
        key_store,
        key_rows,
        value_store,
        value_rows,
        hidden_rows,
        token_owner.reshape(1, store_count),
        owner.reshape(row_count, 1),
        owner.reshape(1, row_count),
    )


def ffn_kernel(rows_ref, gate_ref, up_ref, down_ref, out_ref):
    rows = rows_ref[...]
    gate_value = jnp.dot(rows, gate_ref[...], preferred_element_type=jnp.float32)
    up_value = jnp.dot(rows, up_ref[...], preferred_element_type=jnp.float32)
    hidden = (gate_value / (1.0 + jnp.exp(-gate_value)) * up_value).astype(jnp.bfloat16)
    out_ref[...] = jnp.dot(hidden, down_ref[...], preferred_element_type=jnp.float32).astype(
        out_ref.dtype
    )


def expert_ffn(rows, gate, up, down):
    count, width = rows.shape
    units = gate.shape[1]
    tile = 512
    fixed = lambda shape: pl.BlockSpec(shape, lambda i: (0, 0))
    return pl.pallas_call(
        ffn_kernel,
        grid=(count // tile,),
        in_specs=[
            pl.BlockSpec((tile, width), lambda i: (i, 0)),
            fixed((width, units)),
            fixed((width, units)),
            fixed((units, width)),
        ],
        out_specs=pl.BlockSpec((tile, width), lambda i: (i, 0)),
        out_shape=jax.ShapeDtypeStruct((count, width), jnp.bfloat16),
        interpret=INTERPRET,
    )(rows, gate, up, down)


def shift_exchange(pieces, groups, sign):
    moved = [pieces[0]]
    for shift in range(1, groups):
        pairs = [(i, (i + sign * shift) % groups) for i in range(groups)]
        moved.append(lax.ppermute(pieces[shift], "ex", pairs))
    return jnp.stack(moved)


def per_device(
    hidden_in,
    queries,
    new_keys,
    new_values,
    key_pool,
    value_pool,
    page_order,
    new_lengths,
    context_lengths,
    route_ids,
    norm_gain,
    router_weight,
    gate_weight,
    up_weight,
    down_weight,
    out_gain,
):
    groups = lax.axis_size("ex")
    local_experts = gate_weight.shape[0]
    width = hidden_in.shape[1]
    row_count = hidden_in.shape[0]
    resid = attend(
        hidden_in,
        queries,
        new_keys,
        new_values,
        key_pool,
        value_pool,
        page_order[0],
        new_lengths[0],
        context_lengths[0],
    )
    normed = rms_scale(resid, norm_gain).astype(jnp.bfloat16)
    route_weights = route_probs(normed, router_weight, route_ids)
    top_count = route_ids.shape[1]
    entries = route_ids.reshape(-1)
    expert_range = jnp.arange(EXPERTS, dtype=jnp.int32)
    onehot = (entries[:, None] == expert_range[None, :]).astype(jnp.int32)
    before = jnp.cumsum(onehot, axis=0) - onehot
    slot_index = jnp.sum(before * onehot, axis=1)
    me = lax.axis_index("ex")
    target = ((entries - me) % groups) * MOST + slot_index
    entry_rows = jnp.arange(entries.shape[0], dtype=jnp.int32) // top_count
    source_row = jnp.zeros((EXPERTS * MOST,), jnp.int32).at[target].set(entry_rows)
    filled = jnp.zeros((EXPERTS * MOST,), jnp.bool_).at[target].set(True)
    outgoing = jnp.where(filled[:, None], normed[source_row], jnp.zeros((), jnp.bfloat16)).reshape(
        EXPERTS, MOST, width
    )
    arrived = shift_exchange(outgoing, groups, 1).reshape(groups * MOST, width)
    arrived_rows = lax.all_gather(arrived, "sh", axis=0, tiled=True)
    partial = expert_ffn(arrived_rows, gate_weight[0], up_weight[0], down_weight[0])
    summed = lax.psum_scatter(partial, "sh", scatter_dimension=0, tiled=True)
    returned = shift_exchange(summed.reshape(groups, MOST, width), groups, -1)
    flat_results = returned.reshape(EXPERTS * MOST, width)
    picked = flat_results[target].reshape(row_count, top_count, width)
    mixed = resid + jnp.sum(route_weights[:, :, None] * picked.astype(jnp.float32), axis=1)
    return rms_scale(mixed, out_gain).astype(jnp.bfloat16)


def solution(mesh):
    placed = (
        P(("ex", "sh"), None),
        P(("ex", "sh"), None),
        P(("ex", "sh"), None),
        P(("ex", "sh"), None),
        P(("ex", "sh"), None),
        P(("ex", "sh"), None),
        P(("ex", "sh"), None),
        P(("ex", "sh"), None),
        P(("ex", "sh"), None),
        P(("ex", "sh"), None),
        P(),
        P(),
        P("ex", None, "sh"),
        P("ex", None, "sh"),
        P("ex", "sh", None),
        P(),
    )
    return jax.shard_map(
        per_device, mesh=mesh, in_specs=placed, out_specs=P(("ex", "sh"), None), check_vma=False
    )
```

```python
import jax
import jax.numpy as jnp
from jax import lax
from jax.sharding import PartitionSpec as P
from jax.experimental import pallas as pl

HEADS = 36
HEAD_DIM = 64
EXPERTS = 8
PAGE = 16
MOST = 32
INTERPRET = False


def rms_scale(values, gain):
    mean_square = jnp.mean(values * values, axis=-1, keepdims=True)
    return values * lax.rsqrt(mean_square + 1e-05) * gain.astype(jnp.float32)


def route_probs(normed, router_weight, route_ids):
    logits = jnp.dot(normed, router_weight, preferred_element_type=jnp.float32)
    expert_range = jnp.arange(router_weight.shape[1], dtype=jnp.int32)
    picked = jnp.sum(
        jnp.where(route_ids[:, :, None] == expert_range[None, None, :], logits[:, None, :], 0.0),
        axis=2,
    )
    raised = jnp.exp(picked)
    return raised / jnp.sum(raised, axis=1, keepdims=True)


def attention_kernel(
    query_ref, pool_key_ref, new_key_ref, pool_value_ref, new_value_ref, hidden_ref,
    token_owner_ref, owner_ref, owner_row_ref, out_ref
):
    query = query_ref[...]
    rows = query.shape[0]
    owner = owner_ref[...]
    pool_ok = owner == token_owner_ref[...]
    row_at = lax.broadcasted_iota(jnp.int32, (rows, rows), 0)
    col_at = lax.broadcasted_iota(jnp.int32, (rows, rows), 1)
    new_ok = (owner == owner_row_ref[...]) & (col_at <= row_at)
    lane = lax.broadcasted_iota(jnp.int32, (1, query.shape[1]), 1)
    contract = (((1,), (1,)), ((), ()))
    total = hidden_ref[...].astype(jnp.float32)
    for head in range(query.shape[1] // HEAD_DIM):
        in_head = (lane >= head * HEAD_DIM) & (lane < (head + 1) * HEAD_DIM)
        head_query = jnp.where(in_head, query, jnp.zeros((), query.dtype))
        pool_score = lax.dot_general(
            head_query, pool_key_ref[...], contract, preferred_element_type=jnp.float32
        ) * HEAD_DIM ** (-0.5)
        new_score = lax.dot_general(
            head_query, new_key_ref[...], contract, preferred_element_type=jnp.float32
        ) * HEAD_DIM ** (-0.5)
        pool_raised = jnp.where(pool_ok, jnp.exp(pool_score), 0.0)
        new_raised = jnp.where(new_ok, jnp.exp(new_score), 0.0)
        denom = jnp.sum(pool_raised, axis=1, keepdims=True) + jnp.sum(
            new_raised, axis=1, keepdims=True
        )
        pool_weight = (pool_raised / denom).astype(jnp.bfloat16)
        new_weight = (new_raised / denom).astype(jnp.bfloat16)
        mixed = jnp.dot(
            pool_weight, pool_value_ref[...], preferred_element_type=jnp.float32
        ) + jnp.dot(new_weight, new_value_ref[...], preferred_element_type=jnp.float32)
        total = total + jnp.where(in_head, mixed, 0.0)
    out_ref[...] = total


def attend(
    hidden_rows,
    query_rows,
    key_rows,
    value_rows,
    key_store,
    value_store,
    page_row,
    new_row_lengths,
    context_row_lengths,
):
    row_count, width = query_rows.shape
    store_count = key_store.shape[0]
    requests = new_row_lengths.shape[0]
    per_request = page_row.shape[0] // requests
    ends = jnp.cumsum(new_row_lengths)
    row_index = jnp.arange(row_count, dtype=jnp.int32)
    owner = jnp.sum((row_index[:, None] >= ends[None, :]).astype(jnp.int32), axis=1)
    entry = jnp.arange(page_row.shape[0], dtype=jnp.int32)
    token_index = jnp.arange(store_count, dtype=jnp.int32)
    hit = page_row[:, None] == (token_index // PAGE)[None, :]
    token_entry = jnp.sum(jnp.where(hit, entry[:, None], 0), axis=0)
    token_request = token_entry // per_request
    position = (token_entry % per_request) * PAGE + token_index % PAGE
    request_index = jnp.arange(requests, dtype=jnp.int32)
    limit = jnp.sum(
        jnp.where(
            token_request[None, :] == request_index[:, None], context_row_lengths[:, None], 0
        ),
        axis=0,
    )
    token_owner = jnp.where(position < limit, token_request, -1).astype(jnp.int32)
    block = 2 * HEAD_DIM
    column = lambda count: pl.BlockSpec((count, block), lambda j: (0, j))
    whole = lambda shape: pl.BlockSpec(shape, lambda j: (0, 0))
    return pl.pallas_call(
        attention_kernel,
        grid=(width // block,),
        in_specs=[
            column(row_count),
            column(store_count),
            column(row_count),
            column(store_count),
            column(row_count),
            column(row_count),
            whole((1, store_count)),
            whole((row_count, 1)),
            whole((1, row_count)),
        ],
        out_specs=column(row_count),
        out_shape=jax.ShapeDtypeStruct((row_count, width), jnp.float32),
        interpret=INTERPRET,
    )(
        query_rows,
        key_store,
        key_rows,
        value_store,
        value_rows,
        hidden_rows,
        token_owner.reshape(1, store_count),
        owner.reshape(row_count, 1),
        owner.reshape(1, row_count),
    )


def ffn_kernel(rows_ref, gate_ref, up_ref, down_ref, out_ref):
    rows = rows_ref[...]
    contract = (((1,), (1,)), ((), ()))
    gate_value = lax.dot_general(rows, gate_ref[...], contract, preferred_element_type=jnp.float32)
    up_value = lax.dot_general(rows, up_ref[...], contract, preferred_element_type=jnp.float32)
    hidden = (gate_value / (1.0 + jnp.exp(-gate_value)) * up_value).astype(jnp.bfloat16)
    out_ref[...] = jnp.dot(hidden, down_ref[...], preferred_element_type=jnp.float32).astype(
        out_ref.dtype
    )


def expert_ffn(rows, gate, up, down):
    count, width = rows.shape
    units = gate.shape[0]
    tile = 512
    fixed = lambda shape: pl.BlockSpec(shape, lambda i: (0, 0))
    return pl.pallas_call(
        ffn_kernel,
        grid=(count // tile,),
        in_specs=[
            pl.BlockSpec((tile, width), lambda i: (i, 0)),
            fixed((units, width)),
            fixed((units, width)),
            fixed((units, width)),
        ],
        out_specs=pl.BlockSpec((tile, width), lambda i: (i, 0)),
        out_shape=jax.ShapeDtypeStruct((count, width), jnp.bfloat16),
        interpret=INTERPRET,
    )(rows, gate, up, down)


def per_device(
    hidden_in,
    queries,
    new_keys,
    new_values,
    key_pool,
    value_pool,
    page_order,
    new_lengths,
    context_lengths,
    route_ids,
    norm_gain,
    router_weight,
    gate_weight,
    up_weight,
    down_weight,
    out_gain,
):
    groups = lax.axis_size("ex")
    local_experts = gate_weight.shape[0]
    width = hidden_in.shape[1]
    row_count = hidden_in.shape[0]
    resid = attend(
        hidden_in,
        queries,
        new_keys,
        new_values,
        key_pool,
        value_pool,
        page_order[0],
        new_lengths[0],
        context_lengths[0],
    )
    normed = rms_scale(resid, norm_gain).astype(jnp.bfloat16)
    route_weights = route_probs(normed, router_weight, route_ids)
    top_count = route_ids.shape[1]
    entries = route_ids.reshape(-1)
    expert_range = jnp.arange(EXPERTS, dtype=jnp.int32)
    onehot = (entries[:, None] == expert_range[None, :]).astype(jnp.int32)
    before = jnp.cumsum(onehot, axis=0) - onehot
    slot_index = jnp.sum(before * onehot, axis=1)
    target = entries * MOST + slot_index
    entry_rows = jnp.arange(entries.shape[0], dtype=jnp.int32) // top_count
    source_row = jnp.zeros((EXPERTS * MOST,), jnp.int32).at[target].set(entry_rows)
    filled = jnp.zeros((EXPERTS * MOST,), jnp.bool_).at[target].set(True)
    outgoing = jnp.where(filled[:, None], normed[source_row], jnp.zeros((), jnp.bfloat16)).reshape(
        EXPERTS, MOST, width
    )
    arrived = lax.all_to_all(outgoing, "ex", split_axis=0, concat_axis=0, tiled=True).reshape(
        groups * MOST, width
    )
    arrived_rows = lax.all_gather(arrived, "sh", axis=0, tiled=True)
    partial = expert_ffn(arrived_rows, gate_weight[0].T, up_weight[0].T, down_weight[0])
    summed = lax.psum_scatter(partial, "sh", scatter_dimension=0, tiled=True)
    returned = lax.all_to_all(
        summed.reshape(EXPERTS, MOST, width), "ex", split_axis=0, concat_axis=0, tiled=True
    )
    flat_results = returned.reshape(EXPERTS * MOST, width)
    picked = flat_results[target].reshape(row_count, top_count, width)
    mixed = resid + jnp.sum(route_weights[:, :, None] * picked.astype(jnp.float32), axis=1)
    return rms_scale(mixed, out_gain).astype(jnp.bfloat16)


def solution(mesh):
    placed = (
        P(("ex", "sh"), None),
        P(("ex", "sh"), None),
        P(("ex", "sh"), None),
        P(("ex", "sh"), None),
        P(("ex", "sh"), None),
        P(("ex", "sh"), None),
        P(("ex", "sh"), None),
        P(("ex", "sh"), None),
        P(("ex", "sh"), None),
        P(("ex", "sh"), None),
        P(),
        P(),
        P("ex", None, "sh"),
        P("ex", None, "sh"),
        P("ex", "sh", None),
        P(),
    )
    return jax.shard_map(
        per_device, mesh=mesh, in_specs=placed, out_specs=P(("ex", "sh"), None), check_vma=False
    )
```

```python
import jax
import jax.numpy as jnp
from jax import lax
from jax.sharding import PartitionSpec as P
from jax.experimental import pallas as pl

HEADS = 36
HEAD_DIM = 64
EXPERTS = 8
PAGE = 16
MOST = 32
INTERPRET = False


def rms_scale(values, gain):
    mean_square = jnp.mean(values * values, axis=-1, keepdims=True)
    return values * lax.rsqrt(mean_square + 1e-05) * gain.astype(jnp.float32)


def route_probs(normed, router_weight, route_ids):
    logits = jnp.dot(normed, router_weight, preferred_element_type=jnp.float32)
    expert_range = jnp.arange(router_weight.shape[1], dtype=jnp.int32)
    picked = jnp.sum(
        jnp.where(route_ids[:, :, None] == expert_range[None, None, :], logits[:, None, :], 0.0),
        axis=2,
    )
    raised = jnp.exp(picked)
    return raised / jnp.sum(raised, axis=1, keepdims=True)


def attention_kernel(
    query_ref, pool_key_ref, new_key_ref, pool_value_ref, new_value_ref, hidden_ref,
    token_owner_ref, owner_ref, owner_row_ref, out_ref
):
    query = query_ref[...]
    rows = query.shape[0]
    owner = owner_ref[...]
    pool_ok = owner == token_owner_ref[...]
    row_at = lax.broadcasted_iota(jnp.int32, (rows, rows), 0)
    col_at = lax.broadcasted_iota(jnp.int32, (rows, rows), 1)
    new_ok = (owner == owner_row_ref[...]) & (col_at <= row_at)
    lane = lax.broadcasted_iota(jnp.int32, (1, query.shape[1]), 1)
    contract = (((1,), (1,)), ((), ()))
    total = hidden_ref[...].astype(jnp.float32)
    for head in range(query.shape[1] // HEAD_DIM):
        in_head = (lane >= head * HEAD_DIM) & (lane < (head + 1) * HEAD_DIM)
        head_query = jnp.where(in_head, query, jnp.zeros((), query.dtype))
        pool_score = lax.dot_general(
            head_query, pool_key_ref[...], contract, preferred_element_type=jnp.float32
        ) * HEAD_DIM ** (-0.5)
        new_score = lax.dot_general(
            head_query, new_key_ref[...], contract, preferred_element_type=jnp.float32
        ) * HEAD_DIM ** (-0.5)
        pool_raised = jnp.where(pool_ok, jnp.exp(pool_score), 0.0)
        new_raised = jnp.where(new_ok, jnp.exp(new_score), 0.0)
        denom = jnp.sum(pool_raised, axis=1, keepdims=True) + jnp.sum(
            new_raised, axis=1, keepdims=True
        )
        pool_weight = (pool_raised / denom).astype(jnp.bfloat16)
        new_weight = (new_raised / denom).astype(jnp.bfloat16)
        mixed = jnp.dot(
            pool_weight, pool_value_ref[...], preferred_element_type=jnp.float32
        ) + jnp.dot(new_weight, new_value_ref[...], preferred_element_type=jnp.float32)
        total = total + jnp.where(in_head, mixed, 0.0)
    out_ref[...] = total


def attend(
    hidden_rows,
    query_rows,
    key_rows,
    value_rows,
    key_store,
    value_store,
    page_row,
    new_row_lengths,
    context_row_lengths,
):
    row_count, width = query_rows.shape
    store_count = key_store.shape[0]
    requests = new_row_lengths.shape[0]
    per_request = page_row.shape[0] // requests
    ends = jnp.cumsum(new_row_lengths)
    row_index = jnp.arange(row_count, dtype=jnp.int32)
    owner = jnp.sum((row_index[:, None] >= ends[None, :]).astype(jnp.int32), axis=1)
    entry = jnp.arange(page_row.shape[0], dtype=jnp.int32)
    token_index = jnp.arange(store_count, dtype=jnp.int32)
    hit = page_row[:, None] == (token_index // PAGE)[None, :]
    token_entry = jnp.sum(jnp.where(hit, entry[:, None], 0), axis=0)
    token_request = token_entry // per_request
    position = (token_entry % per_request) * PAGE + token_index % PAGE
    request_index = jnp.arange(requests, dtype=jnp.int32)
    limit = jnp.sum(
        jnp.where(
            token_request[None, :] == request_index[:, None], context_row_lengths[:, None], 0
        ),
        axis=0,
    )
    token_owner = jnp.where(position < limit, token_request, -1).astype(jnp.int32)
    block = 4 * HEAD_DIM
    column = lambda count: pl.BlockSpec((count, block), lambda j: (0, j))
    whole = lambda shape: pl.BlockSpec(shape, lambda j: (0, 0))
    return pl.pallas_call(
        attention_kernel,
        grid=(width // block,),
        in_specs=[
            column(row_count),
            column(store_count),
            column(row_count),
            column(store_count),
            column(row_count),
            column(row_count),
            whole((1, store_count)),
            whole((row_count, 1)),
            whole((1, row_count)),
        ],
        out_specs=column(row_count),
        out_shape=jax.ShapeDtypeStruct((row_count, width), jnp.float32),
        interpret=INTERPRET,
    )(
        query_rows,
        key_store,
        key_rows,
        value_store,
        value_rows,
        hidden_rows,
        token_owner.reshape(1, store_count),
        owner.reshape(row_count, 1),
        owner.reshape(1, row_count),
    )


def ffn_kernel(rows_ref, gate_ref, up_ref, down_ref, out_ref):
    rows = rows_ref[...]
    contract = (((1,), (1,)), ((), ()))
    gate_value = lax.dot_general(rows, gate_ref[...], contract, preferred_element_type=jnp.float32)
    up_value = lax.dot_general(rows, up_ref[...], contract, preferred_element_type=jnp.float32)
    hidden = (gate_value / (1.0 + jnp.exp(-gate_value)) * up_value).astype(jnp.bfloat16)
    out_ref[...] = jnp.dot(hidden, down_ref[...], preferred_element_type=jnp.float32).astype(
        out_ref.dtype
    )


def expert_ffn(rows, gate, up, down):
    count, width = rows.shape
    units = gate.shape[0]
    tile = 1024
    fixed = lambda shape: pl.BlockSpec(shape, lambda i: (0, 0))
    return pl.pallas_call(
        ffn_kernel,
        grid=(count // tile,),
        in_specs=[
            pl.BlockSpec((tile, width), lambda i: (i, 0)),
            fixed((units, width)),
            fixed((units, width)),
            fixed((units, width)),
        ],
        out_specs=pl.BlockSpec((tile, width), lambda i: (i, 0)),
        out_shape=jax.ShapeDtypeStruct((count, width), jnp.bfloat16),
        interpret=INTERPRET,
    )(rows, gate, up, down)


def per_device(
    hidden_in,
    queries,
    new_keys,
    new_values,
    key_pool,
    value_pool,
    page_order,
    new_lengths,
    context_lengths,
    route_ids,
    norm_gain,
    router_weight,
    gate_weight,
    up_weight,
    down_weight,
    out_gain,
):
    groups = lax.axis_size("ex")
    local_experts = gate_weight.shape[0]
    width = hidden_in.shape[1]
    row_count = hidden_in.shape[0]
    resid = attend(
        hidden_in,
        queries,
        new_keys,
        new_values,
        key_pool,
        value_pool,
        page_order[0],
        new_lengths[0],
        context_lengths[0],
    )
    normed = rms_scale(resid, norm_gain).astype(jnp.bfloat16)
    route_weights = route_probs(normed, router_weight, route_ids)
    top_count = route_ids.shape[1]
    entries = route_ids.reshape(-1)
    expert_range = jnp.arange(EXPERTS, dtype=jnp.int32)
    onehot = (entries[:, None] == expert_range[None, :]).astype(jnp.int32)
    before = jnp.cumsum(onehot, axis=0) - onehot
    slot_index = jnp.sum(before * onehot, axis=1)
    target = entries * MOST + slot_index
    entry_rows = jnp.arange(entries.shape[0], dtype=jnp.int32) // top_count
    source_row = jnp.zeros((EXPERTS * MOST,), jnp.int32).at[target].set(entry_rows)
    filled = jnp.zeros((EXPERTS * MOST,), jnp.bool_).at[target].set(True)
    outgoing = jnp.where(filled[:, None], normed[source_row], jnp.zeros((), jnp.bfloat16)).reshape(
        EXPERTS, MOST, width
    )
    arrived = lax.all_to_all(outgoing, "ex", split_axis=0, concat_axis=0, tiled=True).reshape(
        groups * MOST, width
    )
    arrived_rows = lax.all_gather(arrived, "sh", axis=0, tiled=True)
    partial = expert_ffn(arrived_rows, gate_weight[0].T, up_weight[0].T, down_weight[0])
    summed = lax.psum_scatter(partial, "sh", scatter_dimension=0, tiled=True)
    returned = lax.all_to_all(
        summed.reshape(EXPERTS, MOST, width), "ex", split_axis=0, concat_axis=0, tiled=True
    )
    flat_results = returned.reshape(EXPERTS * MOST, width)
    picked = flat_results[target].reshape(row_count, top_count, width)
    mixed = resid + jnp.sum(route_weights[:, :, None] * picked.astype(jnp.float32), axis=1)
    return rms_scale(mixed, out_gain).astype(jnp.bfloat16)


def solution(mesh):
    placed = (
        P(("ex", "sh"), None),
        P(("ex", "sh"), None),
        P(("ex", "sh"), None),
        P(("ex", "sh"), None),
        P(("ex", "sh"), None),
        P(("ex", "sh"), None),
        P(("ex", "sh"), None),
        P(("ex", "sh"), None),
        P(("ex", "sh"), None),
        P(("ex", "sh"), None),
        P(),
        P(),
        P("ex", None, "sh"),
        P("ex", None, "sh"),
        P("ex", "sh", None),
        P(),
    )
    return jax.shard_map(
        per_device, mesh=mesh, in_specs=placed, out_specs=P(("ex", "sh"), None), check_vma=False
    )
```

```python
import jax
import jax.numpy as jnp
from jax import lax
from jax.sharding import PartitionSpec as P
from jax.experimental import pallas as pl

HEADS = 36
HEAD_DIM = 64
EXPERTS = 8
PAGE = 16
MOST = 32
INTERPRET = False


def rms_scale(values, gain):
    mean_square = jnp.mean(values * values, axis=-1, keepdims=True)
    return values * lax.rsqrt(mean_square + 1e-05) * gain.astype(jnp.float32)


def route_probs(normed, router_weight, route_ids):
    logits = jnp.dot(normed, router_weight, preferred_element_type=jnp.float32)
    expert_range = jnp.arange(router_weight.shape[1], dtype=jnp.int32)
    picked = jnp.sum(
        jnp.where(route_ids[:, :, None] == expert_range[None, None, :], logits[:, None, :], 0.0),
        axis=2,
    )
    raised = jnp.exp(picked)
    return raised / jnp.sum(raised, axis=1, keepdims=True)


def attention_kernel(
    query_ref, pool_key_ref, new_key_ref, pool_value_ref, new_value_ref, hidden_ref,
    token_owner_ref, owner_ref, owner_row_ref, out_ref
):
    query = query_ref[...]
    rows = query.shape[0]
    owner = owner_ref[...]
    pool_ok = owner == token_owner_ref[...]
    row_at = lax.broadcasted_iota(jnp.int32, (rows, rows), 0)
    col_at = lax.broadcasted_iota(jnp.int32, (rows, rows), 1)
    new_ok = (owner == owner_row_ref[...]) & (col_at <= row_at)
    lane = lax.broadcasted_iota(jnp.int32, (1, query.shape[1]), 1)
    contract = (((1,), (1,)), ((), ()))
    total = hidden_ref[...].astype(jnp.float32)
    for head in range(query.shape[1] // HEAD_DIM):
        in_head = (lane >= head * HEAD_DIM) & (lane < (head + 1) * HEAD_DIM)
        head_query = jnp.where(in_head, query, jnp.zeros((), query.dtype))
        pool_score = lax.dot_general(
            head_query, pool_key_ref[...], contract, preferred_element_type=jnp.float32
        ) * HEAD_DIM ** (-0.5)
        new_score = lax.dot_general(
            head_query, new_key_ref[...], contract, preferred_element_type=jnp.float32
        ) * HEAD_DIM ** (-0.5)
        pool_raised = jnp.where(pool_ok, jnp.exp(pool_score), 0.0)
        new_raised = jnp.where(new_ok, jnp.exp(new_score), 0.0)
        denom = jnp.sum(pool_raised, axis=1, keepdims=True) + jnp.sum(
            new_raised, axis=1, keepdims=True
        )
        pool_weight = (pool_raised / denom).astype(jnp.bfloat16)
        new_weight = (new_raised / denom).astype(jnp.bfloat16)
        mixed = jnp.dot(
            pool_weight, pool_value_ref[...], preferred_element_type=jnp.float32
        ) + jnp.dot(new_weight, new_value_ref[...], preferred_element_type=jnp.float32)
        total = total + jnp.where(in_head, mixed, 0.0)
    out_ref[...] = total


def attend(
    hidden_rows,
    query_rows,
    key_rows,
    value_rows,
    key_store,
    value_store,
    page_row,
    new_row_lengths,
    context_row_lengths,
):
    row_count, width = query_rows.shape
    store_count = key_store.shape[0]
    requests = new_row_lengths.shape[0]
    per_request = page_row.shape[0] // requests
    ends = jnp.cumsum(new_row_lengths)
    row_index = jnp.arange(row_count, dtype=jnp.int32)
    owner = jnp.sum((row_index[:, None] >= ends[None, :]).astype(jnp.int32), axis=1)
    entry = jnp.arange(page_row.shape[0], dtype=jnp.int32)
    token_index = jnp.arange(store_count, dtype=jnp.int32)
    hit = page_row[:, None] == (token_index // PAGE)[None, :]
    token_entry = jnp.sum(jnp.where(hit, entry[:, None], 0), axis=0)
    token_request = token_entry // per_request
    position = (token_entry % per_request) * PAGE + token_index % PAGE
    request_index = jnp.arange(requests, dtype=jnp.int32)
    limit = jnp.sum(
        jnp.where(
            token_request[None, :] == request_index[:, None], context_row_lengths[:, None], 0
        ),
        axis=0,
    )
    token_owner = jnp.where(position < limit, token_request, -1).astype(jnp.int32)
    block = 2 * HEAD_DIM
    column = lambda count: pl.BlockSpec((count, block), lambda j: (0, j))
    whole = lambda shape: pl.BlockSpec(shape, lambda j: (0, 0))
    return pl.pallas_call(
        attention_kernel,
        grid=(width // block,),
        in_specs=[
            column(row_count),
            column(store_count),
            column(row_count),
            column(store_count),
            column(row_count),
            column(row_count),
            whole((1, store_count)),
            whole((row_count, 1)),
            whole((1, row_count)),
        ],
        out_specs=column(row_count),
        out_shape=jax.ShapeDtypeStruct((row_count, width), jnp.float32),
        interpret=INTERPRET,
    )(
        query_rows,
        key_store,
        key_rows,
        value_store,
        value_rows,
        hidden_rows,
        token_owner.reshape(1, store_count),
        owner.reshape(row_count, 1),
        owner.reshape(1, row_count),
    )


def ffn_kernel(rows_ref, gate_ref, up_ref, down_ref, out_ref):
    rows = rows_ref[...]
    contract = (((1,), (1,)), ((), ()))
    gate_value = lax.dot_general(rows, gate_ref[...], contract, preferred_element_type=jnp.float32)
    up_value = lax.dot_general(rows, up_ref[...], contract, preferred_element_type=jnp.float32)
    hidden = (gate_value / (1.0 + jnp.exp(-gate_value)) * up_value).astype(jnp.bfloat16)
    out_ref[...] = jnp.dot(hidden, down_ref[...], preferred_element_type=jnp.float32).astype(
        out_ref.dtype
    )


def expert_ffn(rows, gate, up, down):
    count, width = rows.shape
    units = gate.shape[0]
    tile = 512
    fixed = lambda shape: pl.BlockSpec(shape, lambda i: (0, 0))
    return pl.pallas_call(
        ffn_kernel,
        grid=(count // tile,),
        in_specs=[
            pl.BlockSpec((tile, width), lambda i: (i, 0)),
            fixed((units, width)),
            fixed((units, width)),
            fixed((units, width)),
        ],
        out_specs=pl.BlockSpec((tile, width), lambda i: (i, 0)),
        out_shape=jax.ShapeDtypeStruct((count, width), jnp.bfloat16),
        interpret=INTERPRET,
    )(rows, gate, up, down)


def per_device(
    hidden_in,
    queries,
    new_keys,
    new_values,
    key_pool,
    value_pool,
    page_order,
    new_lengths,
    context_lengths,
    route_ids,
    norm_gain,
    router_weight,
    gate_weight,
    up_weight,
    down_weight,
    out_gain,
):
    groups = lax.axis_size("ex")
    local_experts = gate_weight.shape[0]
    width = hidden_in.shape[1]
    row_count = hidden_in.shape[0]
    resid = attend(
        hidden_in,
        queries,
        new_keys,
        new_values,
        key_pool,
        value_pool,
        page_order[0],
        new_lengths[0],
        context_lengths[0],
    )
    normed = rms_scale(resid, norm_gain).astype(jnp.bfloat16)
    route_weights = route_probs(normed, router_weight, route_ids)
    top_count = route_ids.shape[1]
    entries = route_ids.reshape(-1)
    expert_range = jnp.arange(EXPERTS, dtype=jnp.int32)
    onehot = (entries[:, None] == expert_range[None, :]).astype(jnp.int32)
    before = jnp.cumsum(onehot, axis=0) - onehot
    slot_index = jnp.sum(before * onehot, axis=1)
    target = entries * MOST + slot_index
    slots = jnp.arange(EXPERTS * MOST, dtype=jnp.int32)
    pick = target.reshape(row_count, top_count)[:, :, None] == slots[None, None, :]
    chosen = jnp.any(pick, axis=1).astype(jnp.bfloat16)
    outgoing = lax.dot_general(
        chosen, normed, (((0,), (0,)), ((), ())), preferred_element_type=jnp.float32
    ).astype(jnp.bfloat16).reshape(EXPERTS, MOST, width)
    arrived = lax.all_to_all(outgoing, "ex", split_axis=0, concat_axis=0, tiled=True).reshape(
        groups * MOST, width
    )
    arrived_rows = lax.all_gather(arrived, "sh", axis=0, tiled=True)
    partial = expert_ffn(arrived_rows, gate_weight[0].T, up_weight[0].T, down_weight[0])
    summed = lax.psum_scatter(partial, "sh", scatter_dimension=0, tiled=True)
    returned = lax.all_to_all(
        summed.reshape(EXPERTS, MOST, width), "ex", split_axis=0, concat_axis=0, tiled=True
    )
    flat_results = returned.reshape(EXPERTS * MOST, width)
    terms = [
        route_weights[:, k : k + 1]
        * jnp.dot(pick[:, k, :].astype(jnp.bfloat16), flat_results, preferred_element_type=jnp.float32)
        for k in range(top_count)
    ]
    mixed = resid + sum(terms[1:], terms[0])
    return rms_scale(mixed, out_gain).astype(jnp.bfloat16)


def solution(mesh):
    placed = (
        P(("ex", "sh"), None),
        P(("ex", "sh"), None),
        P(("ex", "sh"), None),
        P(("ex", "sh"), None),
        P(("ex", "sh"), None),
        P(("ex", "sh"), None),
        P(("ex", "sh"), None),
        P(("ex", "sh"), None),
        P(("ex", "sh"), None),
        P(("ex", "sh"), None),
        P(),
        P(),
        P("ex", None, "sh"),
        P("ex", None, "sh"),
        P("ex", "sh", None),
        P(),
    )
    return jax.shard_map(
        per_device, mesh=mesh, in_specs=placed, out_specs=P(("ex", "sh"), None), check_vma=False
    )
```

```python
import jax
import jax.numpy as jnp
from jax import lax
from jax.sharding import PartitionSpec as P
from jax.experimental import pallas as pl

HEADS = 36
HEAD_DIM = 64
EXPERTS = 8
PAGE = 16
MOST = 32
INTERPRET = False


def rms_scale(values, gain):
    mean_square = jnp.mean(values * values, axis=-1, keepdims=True)
    return values * lax.rsqrt(mean_square + 1e-05) * gain.astype(jnp.float32)


def route_probs(normed, router_weight, route_ids):
    logits = jnp.dot(normed, router_weight, preferred_element_type=jnp.float32)
    expert_range = jnp.arange(router_weight.shape[1], dtype=jnp.int32)
    picked = jnp.sum(
        jnp.where(route_ids[:, :, None] == expert_range[None, None, :], logits[:, None, :], 0.0),
        axis=2,
    )
    raised = jnp.exp(picked)
    return raised / jnp.sum(raised, axis=1, keepdims=True)


def attention_kernel(
    query_ref, pool_key_ref, new_key_ref, pool_value_ref, new_value_ref, hidden_ref,
    token_owner_ref, owner_ref, owner_row_ref, out_ref
):
    query = query_ref[...]
    rows = query.shape[0]
    owner = owner_ref[...]
    pool_ok = owner == token_owner_ref[...]
    row_at = lax.broadcasted_iota(jnp.int32, (rows, rows), 0)
    col_at = lax.broadcasted_iota(jnp.int32, (rows, rows), 1)
    new_ok = (owner == owner_row_ref[...]) & (col_at <= row_at)
    lane = lax.broadcasted_iota(jnp.int32, (1, query.shape[1]), 1)
    contract = (((1,), (1,)), ((), ()))
    total = hidden_ref[...].astype(jnp.float32)
    for head in range(query.shape[1] // HEAD_DIM):
        in_head = (lane >= head * HEAD_DIM) & (lane < (head + 1) * HEAD_DIM)
        head_query = jnp.where(in_head, query, jnp.zeros((), query.dtype))
        pool_score = lax.dot_general(
            head_query, pool_key_ref[...], contract, preferred_element_type=jnp.float32
        ) * HEAD_DIM ** (-0.5)
        new_score = lax.dot_general(
            head_query, new_key_ref[...], contract, preferred_element_type=jnp.float32
        ) * HEAD_DIM ** (-0.5)
        pool_raised = jnp.where(pool_ok, jnp.exp(pool_score), 0.0)
        new_raised = jnp.where(new_ok, jnp.exp(new_score), 0.0)
        denom = jnp.sum(pool_raised, axis=1, keepdims=True) + jnp.sum(
            new_raised, axis=1, keepdims=True
        )
        pool_weight = (pool_raised / denom).astype(jnp.bfloat16)
        new_weight = (new_raised / denom).astype(jnp.bfloat16)
        mixed = jnp.dot(
            pool_weight, pool_value_ref[...], preferred_element_type=jnp.float32
        ) + jnp.dot(new_weight, new_value_ref[...], preferred_element_type=jnp.float32)
        total = total + jnp.where(in_head, mixed, 0.0)
    out_ref[...] = total


def attend(
    hidden_rows,
    query_rows,
    key_rows,
    value_rows,
    key_store,
    value_store,
    page_row,
    new_row_lengths,
    context_row_lengths,
):
    row_count, width = query_rows.shape
    store_count = key_store.shape[0]
    requests = new_row_lengths.shape[0]
    per_request = page_row.shape[0] // requests
    ends = jnp.cumsum(new_row_lengths)
    row_index = jnp.arange(row_count, dtype=jnp.int32)
    owner = jnp.sum((row_index[:, None] >= ends[None, :]).astype(jnp.int32), axis=1)
    entry = jnp.arange(page_row.shape[0], dtype=jnp.int32)
    token_index = jnp.arange(store_count, dtype=jnp.int32)
    hit = page_row[:, None] == (token_index // PAGE)[None, :]
    token_entry = jnp.sum(jnp.where(hit, entry[:, None], 0), axis=0)
    token_request = token_entry // per_request
    position = (token_entry % per_request) * PAGE + token_index % PAGE
    request_index = jnp.arange(requests, dtype=jnp.int32)
    limit = jnp.sum(
        jnp.where(
            token_request[None, :] == request_index[:, None], context_row_lengths[:, None], 0
        ),
        axis=0,
    )
    token_owner = jnp.where(position < limit, token_request, -1).astype(jnp.int32)
    block = 2 * HEAD_DIM
    column = lambda count: pl.BlockSpec((count, block), lambda j: (0, j))
    whole = lambda shape: pl.BlockSpec(shape, lambda j: (0, 0))
    return pl.pallas_call(
        attention_kernel,
        grid=(width // block,),
        in_specs=[
            column(row_count),
            column(store_count),
            column(row_count),
            column(store_count),
            column(row_count),
            column(row_count),
            whole((1, store_count)),
            whole((row_count, 1)),
            whole((1, row_count)),
        ],
        out_specs=column(row_count),
        out_shape=jax.ShapeDtypeStruct((row_count, width), jnp.float32),
        interpret=INTERPRET,
    )(
        query_rows,
        key_store,
        key_rows,
        value_store,
        value_rows,
        hidden_rows,
        token_owner.reshape(1, store_count),
        owner.reshape(row_count, 1),
        owner.reshape(1, row_count),
    )


def ffn_kernel(rows_ref, both_ref, down_ref, out_ref):
    contract = (((1,), (1,)), ((), ()))
    both = lax.dot_general(
        rows_ref[...], both_ref[...], contract, preferred_element_type=jnp.float32
    )
    half = both.shape[1] // 2
    gate_value = both[:, :half]
    up_value = both[:, half:]
    hidden = (gate_value / (1.0 + jnp.exp(-gate_value)) * up_value).astype(jnp.bfloat16)
    out_ref[...] = jnp.dot(hidden, down_ref[...], preferred_element_type=jnp.float32).astype(
        out_ref.dtype
    )


def expert_ffn(rows, gate, up, down):
    count, width = rows.shape
    units = gate.shape[0]
    padded = -(-units // 128) * 128
    spare = ((0, padded - units), (0, 0))
    both = jnp.concatenate([jnp.pad(gate, spare), jnp.pad(up, spare)], axis=0)
    down = jnp.pad(down, spare)
    tile = 512
    fixed = lambda shape: pl.BlockSpec(shape, lambda i: (0, 0))
    return pl.pallas_call(
        ffn_kernel,
        grid=(count // tile,),
        in_specs=[
            pl.BlockSpec((tile, width), lambda i: (i, 0)),
            fixed((2 * padded, width)),
            fixed((padded, width)),
        ],
        out_specs=pl.BlockSpec((tile, width), lambda i: (i, 0)),
        out_shape=jax.ShapeDtypeStruct((count, width), jnp.bfloat16),
        interpret=INTERPRET,
    )(rows, both, down)


def per_device(
    hidden_in,
    queries,
    new_keys,
    new_values,
    key_pool,
    value_pool,
    page_order,
    new_lengths,
    context_lengths,
    route_ids,
    norm_gain,
    router_weight,
    gate_weight,
    up_weight,
    down_weight,
    out_gain,
):
    groups = lax.axis_size("ex")
    local_experts = gate_weight.shape[0]
    width = hidden_in.shape[1]
    row_count = hidden_in.shape[0]
    resid = attend(
        hidden_in,
        queries,
        new_keys,
        new_values,
        key_pool,
        value_pool,
        page_order[0],
        new_lengths[0],
        context_lengths[0],
    )
    normed = rms_scale(resid, norm_gain).astype(jnp.bfloat16)
    route_weights = route_probs(normed, router_weight, route_ids)
    top_count = route_ids.shape[1]
    entries = route_ids.reshape(-1)
    expert_range = jnp.arange(EXPERTS, dtype=jnp.int32)
    onehot = (entries[:, None] == expert_range[None, :]).astype(jnp.int32)
    before = jnp.cumsum(onehot, axis=0) - onehot
    slot_index = jnp.sum(before * onehot, axis=1)
    target = entries * MOST + slot_index
    slots = jnp.arange(EXPERTS * MOST, dtype=jnp.int32)
    pick = target.reshape(row_count, top_count)[:, :, None] == slots[None, None, :]
    chosen = jnp.any(pick, axis=1).astype(jnp.bfloat16)
    outgoing = lax.dot_general(
        chosen, normed, (((0,), (0,)), ((), ())), preferred_element_type=jnp.float32
    ).astype(jnp.bfloat16).reshape(EXPERTS, MOST, width)
    arrived = lax.all_to_all(outgoing, "ex", split_axis=0, concat_axis=0, tiled=True).reshape(
        groups * MOST, width
    )
    arrived_rows = lax.all_gather(arrived, "sh", axis=0, tiled=True)
    partial = expert_ffn(arrived_rows, gate_weight[0].T, up_weight[0].T, down_weight[0])
    summed = lax.psum_scatter(partial, "sh", scatter_dimension=0, tiled=True)
    returned = lax.all_to_all(
        summed.reshape(EXPERTS, MOST, width), "ex", split_axis=0, concat_axis=0, tiled=True
    )
    flat_results = returned.reshape(EXPERTS * MOST, width)
    terms = [
        route_weights[:, k : k + 1]
        * jnp.dot(pick[:, k, :].astype(jnp.bfloat16), flat_results, preferred_element_type=jnp.float32)
        for k in range(top_count)
    ]
    mixed = resid + sum(terms[1:], terms[0])
    return rms_scale(mixed, out_gain).astype(jnp.bfloat16)


def solution(mesh):
    placed = (
        P(("ex", "sh"), None),
        P(("ex", "sh"), None),
        P(("ex", "sh"), None),
        P(("ex", "sh"), None),
        P(("ex", "sh"), None),
        P(("ex", "sh"), None),
        P(("ex", "sh"), None),
        P(("ex", "sh"), None),
        P(("ex", "sh"), None),
        P(("ex", "sh"), None),
        P(),
        P(),
        P("ex", None, "sh"),
        P("ex", None, "sh"),
        P("ex", "sh", None),
        P(),
    )
    return jax.shard_map(
        per_device, mesh=mesh, in_specs=placed, out_specs=P(("ex", "sh"), None), check_vma=False
    )
```

```python
import jax
import jax.numpy as jnp
from jax import lax
from jax.sharding import PartitionSpec as P
from jax.experimental import pallas as pl

HEADS = 36
HEAD_DIM = 64
EXPERTS = 8
PAGE = 16
MOST = 32
INTERPRET = False


def rms_scale(values, gain):
    mean_square = jnp.mean(values * values, axis=-1, keepdims=True)
    return values * lax.rsqrt(mean_square + 1e-05) * gain.astype(jnp.float32)


def route_probs(normed, router_weight, route_ids):
    logits = jnp.dot(normed, router_weight, preferred_element_type=jnp.float32)
    expert_range = jnp.arange(router_weight.shape[1], dtype=jnp.int32)
    picked = jnp.sum(
        jnp.where(route_ids[:, :, None] == expert_range[None, None, :], logits[:, None, :], 0.0),
        axis=2,
    )
    raised = jnp.exp(picked)
    return raised / jnp.sum(raised, axis=1, keepdims=True)


def attention_kernel(
    query_ref, pool_key_ref, new_key_ref, pool_value_ref, new_value_ref, hidden_ref,
    token_owner_ref, owner_ref, owner_row_ref, out_ref
):
    query = query_ref[...]
    rows = query.shape[0]
    owner = owner_ref[...]
    pool_ok = owner == token_owner_ref[...]
    row_at = lax.broadcasted_iota(jnp.int32, (rows, rows), 0)
    col_at = lax.broadcasted_iota(jnp.int32, (rows, rows), 1)
    new_ok = (owner == owner_row_ref[...]) & (col_at <= row_at)
    lane = lax.broadcasted_iota(jnp.int32, (1, query.shape[1]), 1)
    contract = (((1,), (1,)), ((), ()))
    total = hidden_ref[...].astype(jnp.float32)
    for head in range(query.shape[1] // HEAD_DIM):
        in_head = (lane >= head * HEAD_DIM) & (lane < (head + 1) * HEAD_DIM)
        head_query = jnp.where(in_head, query, jnp.zeros((), query.dtype))
        pool_score = lax.dot_general(
            head_query, pool_key_ref[...], contract, preferred_element_type=jnp.float32
        ) * HEAD_DIM ** (-0.5)
        new_score = lax.dot_general(
            head_query, new_key_ref[...], contract, preferred_element_type=jnp.float32
        ) * HEAD_DIM ** (-0.5)
        pool_raised = jnp.where(pool_ok, jnp.exp(pool_score), 0.0)
        new_raised = jnp.where(new_ok, jnp.exp(new_score), 0.0)
        denom = jnp.sum(pool_raised, axis=1, keepdims=True) + jnp.sum(
            new_raised, axis=1, keepdims=True
        )
        pool_weight = (pool_raised / denom).astype(jnp.bfloat16)
        new_weight = (new_raised / denom).astype(jnp.bfloat16)
        mixed = jnp.dot(
            pool_weight, pool_value_ref[...], preferred_element_type=jnp.float32
        ) + jnp.dot(new_weight, new_value_ref[...], preferred_element_type=jnp.float32)
        total = total + jnp.where(in_head, mixed, 0.0)
    out_ref[...] = total


def attend(
    hidden_rows,
    query_rows,
    key_rows,
    value_rows,
    key_store,
    value_store,
    page_row,
    new_row_lengths,
    context_row_lengths,
):
    row_count, width = query_rows.shape
    store_count = key_store.shape[0]
    requests = new_row_lengths.shape[0]
    per_request = page_row.shape[0] // requests
    request_index = jnp.arange(requests, dtype=jnp.int32)
    ends = jnp.sum(
        jnp.where(request_index[None, :] <= request_index[:, None], new_row_lengths[None, :], 0),
        axis=1,
    )
    row_index = jnp.arange(row_count, dtype=jnp.int32)
    owner_column = jnp.sum(
        (row_index[:, None] >= ends[None, :]).astype(jnp.int32), axis=1, keepdims=True
    )
    owner_row = jnp.sum(
        (row_index[None, :] >= ends[:, None]).astype(jnp.int32), axis=0, keepdims=True
    )
    entry = jnp.arange(page_row.shape[0], dtype=jnp.int32)
    token_index = jnp.arange(store_count, dtype=jnp.int32)
    hit = page_row[:, None] == (token_index // PAGE)[None, :]
    token_entry = jnp.sum(jnp.where(hit, entry[:, None], 0), axis=0)
    token_request = token_entry // per_request
    position = (token_entry % per_request) * PAGE + token_index % PAGE
    limit = jnp.sum(
        jnp.where(
            token_request[None, :] == request_index[:, None], context_row_lengths[:, None], 0
        ),
        axis=0,
    )
    token_owner = jnp.where(position < limit, token_request, -1).astype(jnp.int32)
    block = 2 * HEAD_DIM
    column = lambda count: pl.BlockSpec((count, block), lambda j: (0, j))
    whole = lambda shape: pl.BlockSpec(shape, lambda j: (0, 0))
    return pl.pallas_call(
        attention_kernel,
        grid=(width // block,),
        in_specs=[
            column(row_count),
            column(store_count),
            column(row_count),
            column(store_count),
            column(row_count),
            column(row_count),
            whole((1, store_count)),
            whole((row_count, 1)),
            whole((1, row_count)),
        ],
        out_specs=column(row_count),
        out_shape=jax.ShapeDtypeStruct((row_count, width), jnp.float32),
        interpret=INTERPRET,
    )(
        query_rows,
        key_store,
        key_rows,
        value_store,
        value_rows,
        hidden_rows,
        token_owner.reshape(1, store_count),
        owner_column,
        owner_row,
    )


def ffn_kernel(rows_ref, gate_ref, up_ref, down_ref, out_ref):
    rows = rows_ref[...]
    contract = (((1,), (1,)), ((), ()))
    gate_value = lax.dot_general(rows, gate_ref[...], contract, preferred_element_type=jnp.float32)
    up_value = lax.dot_general(rows, up_ref[...], contract, preferred_element_type=jnp.float32)
    hidden = (gate_value / (1.0 + jnp.exp(-gate_value)) * up_value).astype(jnp.bfloat16)
    out_ref[...] = jnp.dot(hidden, down_ref[...], preferred_element_type=jnp.float32).astype(
        out_ref.dtype
    )


def expert_ffn(rows, gate, up, down):
    count, width = rows.shape
    units = gate.shape[0]
    tile = 512
    fixed = lambda shape: pl.BlockSpec(shape, lambda i: (0, 0))
    return pl.pallas_call(
        ffn_kernel,
        grid=(count // tile,),
        in_specs=[
            pl.BlockSpec((tile, width), lambda i: (i, 0)),
            fixed((units, width)),
            fixed((units, width)),
            fixed((units, width)),
        ],
        out_specs=pl.BlockSpec((tile, width), lambda i: (i, 0)),
        out_shape=jax.ShapeDtypeStruct((count, width), jnp.bfloat16),
        interpret=INTERPRET,
    )(rows, gate, up, down)


def per_device(
    hidden_in,
    queries,
    new_keys,
    new_values,
    key_pool,
    value_pool,
    page_order,
    new_lengths,
    context_lengths,
    route_ids,
    norm_gain,
    router_weight,
    gate_weight,
    up_weight,
    down_weight,
    out_gain,
):
    groups = lax.axis_size("ex")
    local_experts = gate_weight.shape[0]
    width = hidden_in.shape[1]
    row_count = hidden_in.shape[0]
    resid = attend(
        hidden_in,
        queries,
        new_keys,
        new_values,
        key_pool,
        value_pool,
        page_order[0],
        new_lengths[0],
        context_lengths[0],
    )
    normed = rms_scale(resid, norm_gain).astype(jnp.bfloat16)
    route_weights = route_probs(normed, router_weight, route_ids)
    top_count = route_ids.shape[1]
    entries = route_ids.reshape(-1)
    expert_range = jnp.arange(EXPERTS, dtype=jnp.int32)
    onehot = (entries[:, None] == expert_range[None, :]).astype(jnp.int32)
    entry_index = jnp.arange(entries.shape[0], dtype=jnp.int32)
    slot_index = jnp.sum(
        (entry_index[None, :] < entry_index[:, None]) & (entries[None, :] == entries[:, None]),
        axis=1,
        dtype=jnp.int32,
    )
    target = entries * MOST + slot_index
    slots = jnp.arange(EXPERTS * MOST, dtype=jnp.int32)
    pick = target.reshape(row_count, top_count)[:, :, None] == slots[None, None, :]
    chosen = jnp.any(pick, axis=1).astype(jnp.bfloat16)
    outgoing = lax.dot_general(
        chosen, normed, (((0,), (0,)), ((), ())), preferred_element_type=jnp.float32
    ).astype(jnp.bfloat16).reshape(EXPERTS, MOST, width)
    arrived = lax.all_to_all(outgoing, "ex", split_axis=0, concat_axis=0, tiled=True).reshape(
        groups * MOST, width
    )
    arrived_rows = lax.all_gather(arrived, "sh", axis=0, tiled=True)
    partial = expert_ffn(arrived_rows, gate_weight[0].T, up_weight[0].T, down_weight[0])
    summed = lax.psum_scatter(partial, "sh", scatter_dimension=0, tiled=True)
    returned = lax.all_to_all(
        summed.reshape(EXPERTS, MOST, width), "ex", split_axis=0, concat_axis=0, tiled=True
    )
    flat_results = returned.reshape(EXPERTS * MOST, width)
    terms = [
        route_weights[:, k : k + 1]
        * jnp.dot(pick[:, k, :].astype(jnp.bfloat16), flat_results, preferred_element_type=jnp.float32)
        for k in range(top_count)
    ]
    mixed = resid + sum(terms[1:], terms[0])
    return rms_scale(mixed, out_gain).astype(jnp.bfloat16)


def solution(mesh):
    placed = (
        P(("ex", "sh"), None),
        P(("ex", "sh"), None),
        P(("ex", "sh"), None),
        P(("ex", "sh"), None),
        P(("ex", "sh"), None),
        P(("ex", "sh"), None),
        P(("ex", "sh"), None),
        P(("ex", "sh"), None),
        P(("ex", "sh"), None),
        P(("ex", "sh"), None),
        P(),
        P(),
        P("ex", None, "sh"),
        P("ex", None, "sh"),
        P("ex", "sh", None),
        P(),
    )
    return jax.shard_map(
        per_device, mesh=mesh, in_specs=placed, out_specs=P(("ex", "sh"), None), check_vma=False
    )
```

```python
import jax
import jax.numpy as jnp
from jax import lax
from jax.sharding import PartitionSpec as P
from jax.experimental import pallas as pl

HEADS = 36
HEAD_DIM = 64
EXPERTS = 8
PAGE = 16
MOST = 32
INTERPRET = False


def rms_scale(values, gain):
    mean_square = jnp.mean(values * values, axis=-1, keepdims=True)
    return values * lax.rsqrt(mean_square + 1e-05) * gain.astype(jnp.float32)


def route_probs(normed, router_weight, route_ids):
    logits = jnp.dot(normed, router_weight, preferred_element_type=jnp.float32)
    expert_range = jnp.arange(router_weight.shape[1], dtype=jnp.int32)
    picked = jnp.sum(
        jnp.where(route_ids[:, :, None] == expert_range[None, None, :], logits[:, None, :], 0.0),
        axis=2,
    )
    raised = jnp.exp(picked)
    return raised / jnp.sum(raised, axis=1, keepdims=True)


def attention_kernel(
    query_ref, pool_key_ref, new_key_ref, pool_value_ref, new_value_ref, hidden_ref,
    token_owner_ref, owner_ref, owner_row_ref, out_ref
):
    query = query_ref[...]
    rows = query.shape[0]
    ends_row = owner_ref[...]
    ends_column = owner_row_ref[...]
    requests = ends_row.shape[1]
    owner = jnp.sum(
        (lax.broadcasted_iota(jnp.int32, (rows, requests), 0) >= ends_row).astype(jnp.int32),
        axis=1,
        keepdims=True,
    )
    owner_row = jnp.sum(
        (lax.broadcasted_iota(jnp.int32, (requests, rows), 1) >= ends_column).astype(jnp.int32),
        axis=0,
        keepdims=True,
    )
    pool_ok = owner == token_owner_ref[...]
    row_at = lax.broadcasted_iota(jnp.int32, (rows, rows), 0)
    col_at = lax.broadcasted_iota(jnp.int32, (rows, rows), 1)
    new_ok = (owner == owner_row) & (col_at <= row_at)
    lane = lax.broadcasted_iota(jnp.int32, (1, query.shape[1]), 1)
    contract = (((1,), (1,)), ((), ()))
    total = hidden_ref[...].astype(jnp.float32)
    for head in range(query.shape[1] // HEAD_DIM):
        in_head = (lane >= head * HEAD_DIM) & (lane < (head + 1) * HEAD_DIM)
        head_query = jnp.where(in_head, query, jnp.zeros((), query.dtype))
        pool_score = lax.dot_general(
            head_query, pool_key_ref[...], contract, preferred_element_type=jnp.float32
        ) * HEAD_DIM ** (-0.5)
        new_score = lax.dot_general(
            head_query, new_key_ref[...], contract, preferred_element_type=jnp.float32
        ) * HEAD_DIM ** (-0.5)
        pool_raised = jnp.where(pool_ok, jnp.exp(pool_score), 0.0)
        new_raised = jnp.where(new_ok, jnp.exp(new_score), 0.0)
        denom = jnp.sum(pool_raised, axis=1, keepdims=True) + jnp.sum(
            new_raised, axis=1, keepdims=True
        )
        pool_weight = (pool_raised / denom).astype(jnp.bfloat16)
        new_weight = (new_raised / denom).astype(jnp.bfloat16)
        mixed = jnp.dot(
            pool_weight, pool_value_ref[...], preferred_element_type=jnp.float32
        ) + jnp.dot(new_weight, new_value_ref[...], preferred_element_type=jnp.float32)
        total = total + jnp.where(in_head, mixed, 0.0)
    out_ref[...] = total


def attend(
    hidden_rows,
    query_rows,
    key_rows,
    value_rows,
    key_store,
    value_store,
    page_row,
    new_row_lengths,
    context_row_lengths,
):
    row_count, width = query_rows.shape
    store_count = key_store.shape[0]
    requests = new_row_lengths.shape[0]
    per_request = page_row.shape[0] // requests
    request_index = jnp.arange(requests, dtype=jnp.int32)
    ends = jnp.sum(
        jnp.where(request_index[None, :] <= request_index[:, None], new_row_lengths[None, :], 0),
        axis=1,
    )
    row_index = jnp.arange(row_count, dtype=jnp.int32)
    entry = jnp.arange(page_row.shape[0], dtype=jnp.int32)
    token_index = jnp.arange(store_count, dtype=jnp.int32)
    hit = page_row[:, None] == (token_index // PAGE)[None, :]
    token_entry = jnp.sum(jnp.where(hit, entry[:, None], 0), axis=0)
    token_request = token_entry // per_request
    position = (token_entry % per_request) * PAGE + token_index % PAGE
    limit = jnp.sum(
        jnp.where(
            token_request[None, :] == request_index[:, None], context_row_lengths[:, None], 0
        ),
        axis=0,
    )
    token_owner = jnp.where(position < limit, token_request, -1).astype(jnp.int32)
    block = 2 * HEAD_DIM
    column = lambda count: pl.BlockSpec((count, block), lambda j: (0, j))
    whole = lambda shape: pl.BlockSpec(shape, lambda j: (0, 0))
    return pl.pallas_call(
        attention_kernel,
        grid=(width // block,),
        in_specs=[
            column(row_count),
            column(store_count),
            column(row_count),
            column(store_count),
            column(row_count),
            column(row_count),
            whole((1, store_count)),
            whole((1, requests)),
            whole((requests, 1)),
        ],
        out_specs=column(row_count),
        out_shape=jax.ShapeDtypeStruct((row_count, width), jnp.float32),
        interpret=INTERPRET,
    )(
        query_rows,
        key_store,
        key_rows,
        value_store,
        value_rows,
        hidden_rows,
        token_owner.reshape(1, store_count),
        ends.reshape(1, requests),
        ends.reshape(requests, 1),
    )


def ffn_kernel(rows_ref, gate_ref, up_ref, down_ref, out_ref):
    rows = rows_ref[...]
    contract = (((1,), (1,)), ((), ()))
    gate_value = lax.dot_general(rows, gate_ref[...], contract, preferred_element_type=jnp.float32)
    up_value = lax.dot_general(rows, up_ref[...], contract, preferred_element_type=jnp.float32)
    hidden = (gate_value / (1.0 + jnp.exp(-gate_value)) * up_value).astype(jnp.bfloat16)
    out_ref[...] = jnp.dot(hidden, down_ref[...], preferred_element_type=jnp.float32).astype(
        out_ref.dtype
    )


def expert_ffn(rows, gate, up, down):
    count, width = rows.shape
    units = gate.shape[0]
    tile = 512
    fixed = lambda shape: pl.BlockSpec(shape, lambda i: (0, 0))
    return pl.pallas_call(
        ffn_kernel,
        grid=(count // tile,),
        in_specs=[
            pl.BlockSpec((tile, width), lambda i: (i, 0)),
            fixed((units, width)),
            fixed((units, width)),
            fixed((units, width)),
        ],
        out_specs=pl.BlockSpec((tile, width), lambda i: (i, 0)),
        out_shape=jax.ShapeDtypeStruct((count, width), jnp.bfloat16),
        interpret=INTERPRET,
    )(rows, gate, up, down)


def per_device(
    hidden_in,
    queries,
    new_keys,
    new_values,
    key_pool,
    value_pool,
    page_order,
    new_lengths,
    context_lengths,
    route_ids,
    norm_gain,
    router_weight,
    gate_weight,
    up_weight,
    down_weight,
    out_gain,
):
    groups = lax.axis_size("ex")
    local_experts = gate_weight.shape[0]
    width = hidden_in.shape[1]
    row_count = hidden_in.shape[0]
    resid = attend(
        hidden_in,
        queries,
        new_keys,
        new_values,
        key_pool,
        value_pool,
        page_order[0],
        new_lengths[0],
        context_lengths[0],
    )
    normed = rms_scale(resid, norm_gain).astype(jnp.bfloat16)
    route_weights = route_probs(normed, router_weight, route_ids)
    top_count = route_ids.shape[1]
    entries = route_ids.reshape(-1)
    expert_range = jnp.arange(EXPERTS, dtype=jnp.int32)
    onehot = (entries[:, None] == expert_range[None, :]).astype(jnp.int32)
    entry_index = jnp.arange(entries.shape[0], dtype=jnp.int32)
    slot_index = jnp.sum(
        (entry_index[None, :] < entry_index[:, None]) & (entries[None, :] == entries[:, None]),
        axis=1,
        dtype=jnp.int32,
    )
    target = entries * MOST + slot_index
    slots = jnp.arange(EXPERTS * MOST, dtype=jnp.int32)
    pick = target.reshape(row_count, top_count)[:, :, None] == slots[None, None, :]
    chosen = jnp.any(pick, axis=1).astype(jnp.bfloat16)
    outgoing = lax.dot_general(
        chosen, normed, (((0,), (0,)), ((), ())), preferred_element_type=jnp.float32
    ).astype(jnp.bfloat16).reshape(EXPERTS, MOST, width)
    arrived = lax.all_to_all(outgoing, "ex", split_axis=0, concat_axis=0, tiled=True).reshape(
        groups * MOST, width
    )
    arrived_rows = lax.all_gather(arrived, "sh", axis=0, tiled=True)
    partial = expert_ffn(arrived_rows, gate_weight[0].T, up_weight[0].T, down_weight[0])
    summed = lax.psum_scatter(partial, "sh", scatter_dimension=0, tiled=True)
    returned = lax.all_to_all(
        summed.reshape(EXPERTS, MOST, width), "ex", split_axis=0, concat_axis=0, tiled=True
    )
    flat_results = returned.reshape(EXPERTS * MOST, width)
    terms = [
        route_weights[:, k : k + 1]
        * jnp.dot(pick[:, k, :].astype(jnp.bfloat16), flat_results, preferred_element_type=jnp.float32)
        for k in range(top_count)
    ]
    mixed = resid + sum(terms[1:], terms[0])
    return rms_scale(mixed, out_gain).astype(jnp.bfloat16)


def solution(mesh):
    placed = (
        P(("ex", "sh"), None),
        P(("ex", "sh"), None),
        P(("ex", "sh"), None),
        P(("ex", "sh"), None),
        P(("ex", "sh"), None),
        P(("ex", "sh"), None),
        P(("ex", "sh"), None),
        P(("ex", "sh"), None),
        P(("ex", "sh"), None),
        P(("ex", "sh"), None),
        P(),
        P(),
        P("ex", None, "sh"),
        P("ex", None, "sh"),
        P("ex", "sh", None),
        P(),
    )
    return jax.shard_map(
        per_device, mesh=mesh, in_specs=placed, out_specs=P(("ex", "sh"), None), check_vma=False
    )
```
